32 devices in a mesh: tm: 16 (over z, y, x), space: 2 (over core).
Axes of the slice: x: 2, y: 2, z: 4, core: 2. Of those that a mesh axis runs over, the one named last changes fastest.
Arguments:
- adjoint: float32 [16, 16, 64, 128], P('tm', 'space'), may hold values from -6 to 6
- base_flow: float32 [3, 16, 16, 64, 128], P(None, 'tm', 'space'), may hold values from -5 to 5
- source: float32 [16, 16, 64, 128], P('tm', 'space'), may hold values from -6 to 6
- pulse: float32 [16], P('tm'), may hold values from 0.3 to 3
- actuator: int32 [16, 128], P('space'), may hold values from 0 to 127
Outputs:
- updated: float32 [16, 16, 64, 128], P('tm', 'space')
- gradient: float32 [128], P('tm')
The draws below stay inside these ranges and needn't reach their ends.
Inputs may be any that keep to these rules, and one draw needn't show every extreme that they name: Each lower-wall cell names the actuator that drives it.
All inputs are finite; a program needn't handle non-finite values.
Results may differ from the reference program's by a relative error of at most 0.00019.
Values sent between devices are 32-bit elements; how exact they have to be, the bound alone decides.
No kernel may reach another device: no remote copies, remote signals or barrier semaphores. Data moves between devices by JAX's collectives and lax.ppermute only.
A program may use at most 64 MiB of HBM per device.

```python
import math
import jax
import jax.numpy as jnp
from jax import lax

NT = 16
CY = 64
CZ = 128
NACT = 128
NX = 16


def place_ends(drawn, rng, low, high):
    spot = [jax.random.randint(jax.random.fold_in(rng, axis), (), 0, length) for axis, length in enumerate(drawn.shape)]
    longest = drawn.shape.index(max(drawn.shape))
    neighbour = spot[:longest] + [(spot[longest] + 1) % drawn.shape[longest]] + spot[longest + 1:]
    return drawn.at[tuple(spot)].set(low).at[tuple(neighbour)].set(high)


def block_scale(key, dims, shards, least, largest):
    loudness = 1.0
    for axis_at, shards_of in shards:
        draws = jax.random.uniform(jax.random.fold_in(jax.random.fold_in(key, 6), axis_at), (shards_of,), jnp.float32, least / len(shards), largest / len(shards))
        loudness = loudness * jnp.repeat(jnp.exp(draws), dims[axis_at] // shards_of).reshape((-1,) + (1,) * (len(dims) - 1 - axis_at))
    return loudness


def scatter_about(rng, dims, scale, limit, pieces=(), kind=jnp.bfloat16):
    gain = block_scale(rng, dims, pieces, -0.22, 0.18) if pieces else 1.0
    array = jax.random.normal(rng, dims, jnp.float32) * scale * gain
    return jnp.minimum(jnp.maximum(array, -limit), limit).astype(kind)


def setup_inputs(seed: int = 0) -> dict:
    keys = jax.random.split(jax.random.key(seed), 6)
    adjoint = scatter_about(keys[0], (NT, NX, CY, CZ), 1.0, 6.0, ((0, 16), (1, 2)), jnp.float32)
    base_flow = scatter_about(keys[1], (3, NT, NX, CY, CZ), 1.0, 5.0, ((1, 16), (2, 2)), jnp.float32)
    source = scatter_about(keys[2], (NT, NX, CY, CZ), 1.0, 6.0, ((0, 16), (1, 2)), jnp.float32)
    pulse = jnp.clip(jnp.exp(math.log(3.0) - 2.3025851 * jax.random.uniform(keys[3], (NT,), jnp.float32) ** block_scale(keys[3], (NT,), ((0, 16),), -0.2, 0.2)), 0.3, 3.0)
    actuator = place_ends(jax.random.randint(keys[4], (NX, CZ), 0, NACT), jax.random.fold_in(keys[4], 1), 0, NACT - 1).astype(jnp.int32)
    return dict(adjoint=adjoint, base_flow=base_flow, source=source, pulse=pulse, actuator=actuator)


omega_rate = 0.25
pseudo_step = 0.2
viscosity = 0.2
reaction = 0.5


def spectral_matrix(count):
    steps = jnp.arange(count, dtype=jnp.int32)
    offset = steps[:, None] - steps[None, :]
    theta = math.pi * offset.astype(jnp.float32) / count
    parity = jnp.where(offset % 2 == 0, 1.0, -1.0).astype(jnp.float32)
    skipped = (offset == 0) | (jnp.abs(offset) == count // 2)
    safe_tan = jnp.where(skipped, jnp.float32(1.0), jnp.tan(theta))
    return jnp.where(skipped, jnp.float32(0.0), 0.5 * parity / safe_tan).astype(jnp.float32)


def wall_plus(field):
    zeros = jnp.zeros_like(field[:, :, :1])
    return jnp.concatenate([field[:, :, 1:], zeros], axis=2)


def wall_minus(field):
    zeros = jnp.zeros_like(field[:, :, :1])
    return jnp.concatenate([zeros, field[:, :, :-1]], axis=2)


def reference(adjoint, base_flow, source, pulse, actuator):
    dmat = spectral_matrix(NT)
    time_term = omega_rate * jnp.einsum("ji,jxyz->ixyz", dmat, adjoint, precision=lax.Precision.HIGHEST)
    flux_x = base_flow[0] * adjoint
    flux_y = base_flow[1] * adjoint
    flux_z = base_flow[2] * adjoint
    advect = 0.5 * (jnp.roll(flux_x, -1, axis=1) - jnp.roll(flux_x, 1, axis=1))
    advect = advect + 0.5 * (wall_plus(flux_y) - wall_minus(flux_y))
    advect = advect + 0.5 * (jnp.roll(flux_z, -1, axis=3) - jnp.roll(flux_z, 1, axis=3))
    beside = jnp.roll(adjoint, -1, axis=1) + jnp.roll(adjoint, 1, axis=1)
    beside = beside + wall_plus(adjoint) + wall_minus(adjoint)
    beside = beside + jnp.roll(adjoint, -1, axis=3) + jnp.roll(adjoint, 1, axis=3)
    operator = advect + viscosity * (beside - 6.0 * adjoint) - reaction * adjoint
    residual = time_term - operator - source
    updated = adjoint - pseudo_step * residual
    wall = updated[:, :, 0, :]
    weighted = jnp.einsum("i,ixz->xz", pulse, wall, precision=lax.Precision.HIGHEST)
    onehot = (actuator[:, :, None] == jnp.arange(NACT, dtype=jnp.int32)[None, None, :]).astype(jnp.float32)
    gradient = jnp.dot(weighted.reshape(1, -1), onehot.reshape(-1, NACT), precision=lax.Precision.HIGHEST, preferred_element_type=jnp.float32)[0] / NT
    return updated, gradient
```

```python
import math

import jax
import jax.numpy as jnp
from jax import lax
from jax.sharding import PartitionSpec as P

NACT = 128


omega_rate = 0.25
pseudo_step = 0.2
viscosity = 0.2
reaction = 0.5


def spectral_matrix(count):
    steps = jnp.arange(count, dtype=jnp.int32)
    offset = steps[:, None] - steps[None, :]
    theta = math.pi * offset.astype(jnp.float32) / count
    parity = jnp.where(offset % 2 == 0, 1.0, -1.0).astype(jnp.float32)
    skipped = (offset == 0) | (jnp.abs(offset) == count // 2)
    safe_tan = jnp.where(skipped, jnp.float32(1.0), jnp.tan(theta))
    return jnp.where(skipped, jnp.float32(0.0), 0.5 * parity / safe_tan).astype(jnp.float32)


def padded(x, sides, width):
    for axis, dim in sides:
        count, length = (lax.axis_size(axis), x.shape[dim])
        up = [(i, (i + 1) % count) for i in range(count)]
        down = [(j, i) for i, j in up]
        last = lax.slice_in_dim(x, length - width, length, axis=dim)
        initial = lax.slice_in_dim(x, 0, width, axis=dim)
        before = lax.ppermute(last, axis, up)
        after = lax.ppermute(initial, axis, down)
        x = jnp.concatenate([before, x, after], axis=dim)
    return x


def wall_plus(field):
    zeros = jnp.zeros_like(field[:, :1])
    return jnp.concatenate([field[:, 1:], zeros], axis=1)


def wall_minus(field):
    zeros = jnp.zeros_like(field[:, :1])
    return jnp.concatenate([zeros, field[:, :-1]], axis=1)


def time_derivative(adjoint):
    count = lax.axis_size("tm")
    nt_loc, nx, cy, cz = adjoint.shape
    total = count * nt_loc
    rows = nx * cy
    chunk = rows // count
    dmat = spectral_matrix(total)
    blocks = adjoint.reshape(nt_loc, count, chunk, cz)
    gathered = lax.all_to_all(blocks, "tm", 1, 0, tiled=False)
    gathered = gathered.reshape(total, chunk * cz)
    derived = omega_rate * jnp.einsum(
        "ji,jp->ip", dmat, gathered, precision=lax.Precision.HIGHEST
    )
    derived = derived.reshape(count, nt_loc, chunk, cz)
    back = lax.all_to_all(derived, "tm", 0, 1, tiled=False)
    return back.reshape(nt_loc, nx, cy, cz)


def on_device(adjoint, base_flow, source, pulse, actuator):
    count = lax.axis_size("tm")
    position = lax.axis_index("tm")
    total = count * adjoint.shape[0]
    time_term = time_derivative(adjoint)[0]
    field = adjoint[0]
    flux_x = base_flow[0, 0] * field
    flux_y = base_flow[1, 0] * field
    flux_z = base_flow[2, 0] * field
    extended = padded(jnp.stack([field, flux_x]), (("space", 1),), 1)
    advect = 0.5 * (extended[1, 2:] - extended[1, :-2])
    advect = advect + 0.5 * (wall_plus(flux_y) - wall_minus(flux_y))
    advect = advect + 0.5 * (jnp.roll(flux_z, -1, axis=2) - jnp.roll(flux_z, 1, axis=2))
    beside = extended[0, 2:] + extended[0, :-2]
    beside = beside + wall_plus(field) + wall_minus(field)
    beside = beside + jnp.roll(field, -1, axis=2) + jnp.roll(field, 1, axis=2)
    operator = advect + viscosity * (beside - 6.0 * field) - reaction * field
    residual = time_term - operator - source[0]
    updated = field - pseudo_step * residual
    wall = updated[:, 0, :] * pulse[0]
    onehot = (actuator[:, :, None] == jnp.arange(NACT, dtype=jnp.int32)[None, None, :]).astype(
        jnp.float32
    )
    partial_sum = (
        jnp.dot(
            wall.reshape(1, -1),
            onehot.reshape(-1, NACT),
            precision=lax.Precision.HIGHEST,
            preferred_element_type=jnp.float32,
        )[0]
        / total
    )
    share = lax.psum_scatter(partial_sum, "tm", scatter_dimension=0, tiled=True)
    gradient = lax.psum(share, "space")
    return (updated[None], gradient)


def solution(mesh):
    in_specs = (
        P("tm", "space", None, None),
        P(None, "tm", "space", None, None),
        P("tm", "space", None, None),
        P("tm"),
        P("space", None),
    )
    out_specs = (P("tm", "space", None, None), P("tm"))
    return jax.shard_map(
        on_device, mesh=mesh, in_specs=in_specs, out_specs=out_specs, check_vma=False
    )
```

```python
import math

import jax
import jax.numpy as jnp
from jax import lax
from jax.sharding import PartitionSpec as P

NACT = 128


omega_rate = 0.25
pseudo_step = 0.2
viscosity = 0.2
reaction = 0.5


def spectral_matrix(count):
    steps = jnp.arange(count, dtype=jnp.int32)
    offset = steps[:, None] - steps[None, :]
    theta = math.pi * offset.astype(jnp.float32) / count
    parity = jnp.where(offset % 2 == 0, 1.0, -1.0).astype(jnp.float32)
    skipped = (offset == 0) | (jnp.abs(offset) == count // 2)
    safe_tan = jnp.where(skipped, jnp.float32(1.0), jnp.tan(theta))
    return jnp.where(skipped, jnp.float32(0.0), 0.5 * parity / safe_tan).astype(jnp.float32)


def padded(x, sides, width):
    for axis, dim in sides:
        count, length = (lax.axis_size(axis), x.shape[dim])
        up = [(i, (i + 1) % count) for i in range(count)]
        down = [(j, i) for i, j in up]
        last = lax.slice_in_dim(x, length - width, length, axis=dim)
        initial = lax.slice_in_dim(x, 0, width, axis=dim)
        before = lax.ppermute(last, axis, up)
        after = lax.ppermute(initial, axis, down)
        x = jnp.concatenate([before, x, after], axis=dim)
    return x


def wall_plus(field):
    zeros = jnp.zeros_like(field[:, :1])
    return jnp.concatenate([field[:, 1:], zeros], axis=1)


def wall_minus(field):
    zeros = jnp.zeros_like(field[:, :1])
    return jnp.concatenate([zeros, field[:, :-1]], axis=1)


def time_derivative(adjoint):
    count = lax.axis_size("tm")
    nt_loc, nx, cy, cz = adjoint.shape
    total = count * nt_loc
    rows = nx * cy
    chunk = rows // count
    dmat = spectral_matrix(total)
    blocks = adjoint.reshape(nt_loc, count, chunk, cz)
    gathered = lax.all_to_all(blocks, "tm", 1, 0, tiled=False)
    gathered = gathered.reshape(total, chunk * cz)
    derived = omega_rate * jnp.einsum(
        "ji,jp->ip", dmat, gathered, precision=lax.Precision.HIGHEST
    )
    derived = derived.reshape(count, nt_loc, chunk, cz)
    back = lax.all_to_all(derived, "tm", 0, 1, tiled=False)
    return back.reshape(nt_loc, nx, cy, cz)


def on_device(adjoint, base_flow, source, pulse, actuator):
    count = lax.axis_size("tm")
    position = lax.axis_index("tm")
    total = count * adjoint.shape[0]
    time_term = time_derivative(adjoint)[0]
    field = adjoint[0]
    flux_x = base_flow[0, 0] * field
    flux_y = base_flow[1, 0] * field
    flux_z = base_flow[2, 0] * field
    extended = padded(jnp.stack([field, flux_x]), (("space", 1),), 1)
    advect = 0.5 * (extended[1, 2:] - extended[1, :-2])
    advect = advect + 0.5 * (wall_plus(flux_y) - wall_minus(flux_y))
    advect = advect + 0.5 * (jnp.roll(flux_z, -1, axis=2) - jnp.roll(flux_z, 1, axis=2))
    beside = extended[0, 2:] + extended[0, :-2]
    beside = beside + wall_plus(field) + wall_minus(field)
    beside = beside + jnp.roll(field, -1, axis=2) + jnp.roll(field, 1, axis=2)
    operator = advect + viscosity * (beside - 6.0 * field) - reaction * field
    residual = time_term - operator - source[0]
    updated = field - pseudo_step * residual
    wall = updated[:, 0, :] * pulse[0]
    onehot = (actuator[:, :, None] == jnp.arange(NACT, dtype=jnp.int32)[None, None, :]).astype(
        jnp.float32
    )
    partial_sum = (
        jnp.dot(
            wall.reshape(1, -1),
            onehot.reshape(-1, NACT),
            precision=lax.Precision.HIGHEST,
            preferred_element_type=jnp.float32,
        )[0]
        / total
    )
    share = NACT // count
    groups = lax.axis_size("space")
    blocks = jnp.repeat(partial_sum.reshape(count, 1, share), groups, axis=1)
    blocks = blocks.reshape(count * groups, share)
    gathered = lax.all_to_all(blocks, ("tm", "space"), 0, 0, tiled=True)
    gradient = jnp.sum(gathered, axis=0)
    return (updated[None], gradient)


def solution(mesh):
    in_specs = (
        P("tm", "space", None, None),
        P(None, "tm", "space", None, None),
        P("tm", "space", None, None),
        P("tm"),
        P("space", None),
    )
    out_specs = (P("tm", "space", None, None), P("tm"))
    return jax.shard_map(
        on_device, mesh=mesh, in_specs=in_specs, out_specs=out_specs, check_vma=False
    )
```

```python
import math

import jax
import jax.numpy as jnp
from jax import lax
from jax.sharding import PartitionSpec as P

NACT = 128


omega_rate = 0.25
pseudo_step = 0.2
viscosity = 0.2
reaction = 0.5


def spectral_matrix(count):
    steps = jnp.arange(count, dtype=jnp.int32)
    offset = steps[:, None] - steps[None, :]
    theta = math.pi * offset.astype(jnp.float32) / count
    parity = jnp.where(offset % 2 == 0, 1.0, -1.0).astype(jnp.float32)
    skipped = (offset == 0) | (jnp.abs(offset) == count // 2)
    safe_tan = jnp.where(skipped, jnp.float32(1.0), jnp.tan(theta))
    return jnp.where(skipped, jnp.float32(0.0), 0.5 * parity / safe_tan).astype(jnp.float32)


def padded(x, sides, width):
    for axis, dim in sides:
        count, length = (lax.axis_size(axis), x.shape[dim])
        up = [(i, (i + 1) % count) for i in range(count)]
        down = [(j, i) for i, j in up]
        last = lax.slice_in_dim(x, length - width, length, axis=dim)
        initial = lax.slice_in_dim(x, 0, width, axis=dim)
        before = lax.ppermute(last, axis, up)
        after = lax.ppermute(initial, axis, down)
        x = jnp.concatenate([before, x, after], axis=dim)
    return x


def wall_plus(field):
    zeros = jnp.zeros_like(field[:, :1])
    return jnp.concatenate([field[:, 1:], zeros], axis=1)


def wall_minus(field):
    zeros = jnp.zeros_like(field[:, :1])
    return jnp.concatenate([zeros, field[:, :-1]], axis=1)


def butterfly_sum(x, axis):
    groups = lax.axis_size(axis)
    bit = 1
    while bit < groups:
        x = x + lax.ppermute(x, axis, [(i, i ^ bit) for i in range(groups)])
        bit *= 2
    return x


def on_device(adjoint, base_flow, source, pulse, actuator):
    count = lax.axis_size("tm")
    position = lax.axis_index("tm")
    nt_loc, nx, cy, cz = adjoint.shape
    total = count * nt_loc
    chunk = nx * cy // count
    share = NACT // count
    dmat = spectral_matrix(total)

    blocks = adjoint.reshape(nt_loc, count, chunk, cz)
    pulse_row = jnp.broadcast_to(pulse.reshape(nt_loc, 1, 1, 1), (nt_loc, count, 1, cz))
    outgoing = jnp.concatenate([blocks, pulse_row], axis=2)
    incoming = lax.all_to_all(outgoing, "tm", 1, 0, tiled=False)
    pulses = incoming[:, :, chunk, 0].reshape(total)
    gathered = incoming[:, :, :chunk].reshape(total, chunk * cz)
    derived = omega_rate * jnp.einsum(
        "ji,jp->ip", dmat, gathered, precision=lax.Precision.HIGHEST
    )

    field = adjoint[0]
    flux_x = base_flow[0, 0] * field
    flux_y = base_flow[1, 0] * field
    flux_z = base_flow[2, 0] * field
    extended = padded(jnp.stack([field, flux_x]), (("space", 1),), 1)
    advect = 0.5 * (extended[1, 2:] - extended[1, :-2])
    advect = advect + 0.5 * (wall_plus(flux_y) - wall_minus(flux_y))
    advect = advect + 0.5 * (jnp.roll(flux_z, -1, axis=2) - jnp.roll(flux_z, 1, axis=2))
    beside = extended[0, 2:] + extended[0, :-2]
    beside = beside + wall_plus(field) + wall_minus(field)
    beside = beside + jnp.roll(field, -1, axis=2) + jnp.roll(field, 1, axis=2)
    operator = advect + viscosity * (beside - 6.0 * field) - reaction * field

    kept = field + pseudo_step * (operator + source[0])
    walls = jnp.stack([pulse[0] * kept[:, 0, :], field[:, 0, :]]).reshape(2, -1)
    onehot = (actuator[:, :, None] == jnp.arange(NACT, dtype=jnp.int32)[None, None, :]).astype(
        jnp.float32
    )
    terms = jnp.dot(
        walls,
        onehot.reshape(-1, NACT),
        precision=lax.Precision.HIGHEST,
        preferred_element_type=jnp.float32,
    )
    terms = butterfly_sum(terms, "space")
    weights = jnp.dot(dmat, pulses, precision=lax.Precision.HIGHEST)
    own_weight = lax.dynamic_index_in_dim(weights, position, keepdims=False)
    partial_sum = (terms[0] - pseudo_step * omega_rate * own_weight * terms[1]) / total
    grad_row = jnp.pad(partial_sum.reshape(count, 1, 1, share), ((0, 0), (0, 0), (0, 0), (0, cz - share)))

    derived = derived.reshape(count, nt_loc, chunk, cz)
    outgoing = jnp.concatenate([derived, grad_row], axis=2)
    incoming = lax.all_to_all(outgoing, "tm", 0, 1, tiled=False)
    time_term = incoming[:, :, :chunk].reshape(nt_loc, nx, cy, cz)[0]
    gradient = jnp.sum(incoming[0, :, chunk, :share], axis=0)

    residual = time_term - operator - source[0]
    updated = field - pseudo_step * residual
    return (updated[None], gradient)


def solution(mesh):
    in_specs = (
        P("tm", "space", None, None),
        P(None, "tm", "space", None, None),
        P("tm", "space", None, None),
        P("tm"),
        P("space", None),
    )
    out_specs = (P("tm", "space", None, None), P("tm"))
    return jax.shard_map(
        on_device, mesh=mesh, in_specs=in_specs, out_specs=out_specs, check_vma=False
    )
```

```python
import math

import jax
import jax.numpy as jnp
from jax import lax
from jax.sharding import PartitionSpec as P

NACT = 128


omega_rate = 0.25
pseudo_step = 0.2
viscosity = 0.2
reaction = 0.5


def spectral_matrix(count):
    steps = jnp.arange(count, dtype=jnp.int32)
    offset = steps[:, None] - steps[None, :]
    theta = math.pi * offset.astype(jnp.float32) / count
    parity = jnp.where(offset % 2 == 0, 1.0, -1.0).astype(jnp.float32)
    skipped = (offset == 0) | (jnp.abs(offset) == count // 2)
    safe_tan = jnp.where(skipped, jnp.float32(1.0), jnp.tan(theta))
    return jnp.where(skipped, jnp.float32(0.0), 0.5 * parity / safe_tan).astype(jnp.float32)


def padded(x, sides, width):
    for axis, dim in sides:
        count, length = (lax.axis_size(axis), x.shape[dim])
        up = [(i, (i + 1) % count) for i in range(count)]
        down = [(j, i) for i, j in up]
        last = lax.slice_in_dim(x, length - width, length, axis=dim)
        initial = lax.slice_in_dim(x, 0, width, axis=dim)
        before = lax.ppermute(last, axis, up)
        after = lax.ppermute(initial, axis, down)
        x = jnp.concatenate([before, x, after], axis=dim)
    return x


def wall_plus(field):
    zeros = jnp.zeros_like(field[:, :1])
    return jnp.concatenate([field[:, 1:], zeros], axis=1)


def wall_minus(field):
    zeros = jnp.zeros_like(field[:, :1])
    return jnp.concatenate([zeros, field[:, :-1]], axis=1)


def butterfly_sum(x, axis):
    groups = lax.axis_size(axis)
    bit = 1
    while bit < groups:
        x = x + lax.ppermute(x, axis, [(i, i ^ bit) for i in range(groups)])
        bit *= 2
    return x


def spectral_row(position, count):
    steps = jnp.arange(count, dtype=jnp.int32)
    offset = position - steps
    theta = math.pi * offset.astype(jnp.float32) / count
    parity = jnp.where(offset % 2 == 0, 1.0, -1.0).astype(jnp.float32)
    skipped = (offset == 0) | (jnp.abs(offset) == count // 2)
    safe_tan = jnp.where(skipped, jnp.float32(1.0), jnp.tan(theta))
    return jnp.where(skipped, jnp.float32(0.0), 0.5 * parity / safe_tan).astype(jnp.float32)


def on_device(adjoint, base_flow, source, pulse, actuator):
    count = lax.axis_size("tm")
    position = lax.axis_index("tm")
    nt_loc, nx, cy, cz = adjoint.shape
    total = count * nt_loc
    chunk = nx * cy // count
    share = NACT // count
    pad = 8
    dmat = spectral_matrix(total)

    blocks = adjoint.reshape(count, chunk, cz)
    pulse_rows = jnp.broadcast_to(pulse.reshape(1, 1, 1), (count, pad, cz))
    outgoing = jnp.concatenate([blocks, pulse_rows], axis=1)
    incoming = lax.all_to_all(outgoing, "tm", 0, 0, tiled=True)
    pulses = incoming[:, chunk, 0]
    gathered = incoming[:, :chunk].reshape(total, chunk * cz)
    derived = omega_rate * jnp.einsum(
        "ji,jp->ip", dmat, gathered, precision=lax.Precision.HIGHEST
    )

    field = adjoint[0]
    flux_x = base_flow[0, 0] * field
    flux_y = base_flow[1, 0] * field
    flux_z = base_flow[2, 0] * field
    extended = padded(jnp.stack([field, flux_x]), (("space", 1),), 1)
    advect = 0.5 * (extended[1, 2:] - extended[1, :-2])
    advect = advect + 0.5 * (wall_plus(flux_y) - wall_minus(flux_y))
    advect = advect + 0.5 * (jnp.roll(flux_z, -1, axis=2) - jnp.roll(flux_z, 1, axis=2))
    beside = extended[0, 2:] + extended[0, :-2]
    beside = beside + wall_plus(field) + wall_minus(field)
    beside = beside + jnp.roll(field, -1, axis=2) + jnp.roll(field, 1, axis=2)
    operator = advect + viscosity * (beside - 6.0 * field) - reaction * field
    forcing = operator + source[0]

    kept = field + pseudo_step * forcing
    walls = jnp.stack([pulse[0] * kept[:, 0, :], field[:, 0, :]]).reshape(2, -1)
    onehot = (actuator[:, :, None] == jnp.arange(NACT, dtype=jnp.int32)[None, None, :]).astype(
        jnp.float32
    )
    terms = jnp.dot(
        walls,
        onehot.reshape(-1, NACT),
        precision=lax.Precision.HIGHEST,
        preferred_element_type=jnp.float32,
    )
    terms = butterfly_sum(terms, "space")
    forcing, terms = lax.optimization_barrier((forcing, terms))
    own_weight = jnp.sum(spectral_row(position, total) * pulses)
    partial_sum = (terms[0] - pseudo_step * omega_rate * own_weight * terms[1]) / total
    grad_rows = jnp.pad(partial_sum.reshape(count, 1, share), ((0, 0), (0, pad - 1), (0, cz - share)))

    outgoing = jnp.concatenate([derived.reshape(count, chunk, cz), grad_rows], axis=1)
    incoming = lax.all_to_all(outgoing, "tm", 0, 0, tiled=True)
    time_term = incoming[:, :chunk].reshape(nx, cy, cz)
    gradient = jnp.sum(incoming[:, chunk, :share], axis=0)

    updated = field - pseudo_step * (time_term - forcing)
    return (updated[None], gradient)


def solution(mesh):
    in_specs = (
        P("tm", "space", None, None),
        P(None, "tm", "space", None, None),
        P("tm", "space", None, None),
        P("tm"),
        P("space", None),
    )
    out_specs = (P("tm", "space", None, None), P("tm"))
    return jax.shard_map(
        on_device, mesh=mesh, in_specs=in_specs, out_specs=out_specs, check_vma=False
    )
```

```python
import math

import jax
import jax.numpy as jnp
from jax import lax
from jax.sharding import PartitionSpec as P

NACT = 128


omega_rate = 0.25
pseudo_step = 0.2
viscosity = 0.2
reaction = 0.5


def spectral_matrix(count):
    steps = jnp.arange(count, dtype=jnp.int32)
    offset = steps[:, None] - steps[None, :]
    theta = math.pi * offset.astype(jnp.float32) / count
    parity = jnp.where(offset % 2 == 0, 1.0, -1.0).astype(jnp.float32)
    skipped = (offset == 0) | (jnp.abs(offset) == count // 2)
    safe_tan = jnp.where(skipped, jnp.float32(1.0), jnp.tan(theta))
    return jnp.where(skipped, jnp.float32(0.0), 0.5 * parity / safe_tan).astype(jnp.float32)


def wall_plus(field):
    zeros = jnp.zeros_like(field[:, :1])
    return jnp.concatenate([field[:, 1:], zeros], axis=1)


def wall_minus(field):
    zeros = jnp.zeros_like(field[:, :1])
    return jnp.concatenate([zeros, field[:, :-1]], axis=1)


def butterfly_sum(x, axis):
    groups = lax.axis_size(axis)
    bit = 1
    while bit < groups:
        x = x + lax.ppermute(x, axis, [(i, i ^ bit) for i in range(groups)])
        bit *= 2
    return x


def halo(ends, axis):
    count = lax.axis_size(axis)
    up = [(i, (i + 1) % count) for i in range(count)]
    down = [(j, i) for i, j in up]
    before = lax.ppermute(ends[1], axis, up)
    after = lax.ppermute(ends[0], axis, down)
    return before, after


def on_device(adjoint, base_flow, source, pulse, actuator):
    count = lax.axis_size("tm")
    nt_loc, nx, cy, cz = adjoint.shape
    total = count * nt_loc
    chunk = nx * cy // count
    share = NACT // count
    pad = 8
    dmat = spectral_matrix(total)

    incoming = lax.all_to_all(adjoint.reshape(count, chunk, cz), "tm", 0, 0, tiled=True)
    derived = omega_rate * jnp.einsum(
        "ji,jp->ip", dmat, incoming.reshape(total, chunk * cz), precision=lax.Precision.HIGHEST
    )

    field = adjoint[0]
    velocity = base_flow[:, 0]
    ends = [jnp.stack([field[k], velocity[0, k] * field[k]]) for k in (0, nx - 1)]
    before, after = halo(ends, "space")
    flux_x = velocity[0] * field
    flux_y = velocity[1] * field
    flux_z = velocity[2] * field
    ahead_x = jnp.concatenate([flux_x[1:], after[1][None]], axis=0)
    behind_x = jnp.concatenate([before[1][None], flux_x[:-1]], axis=0)
    ahead = jnp.concatenate([field[1:], after[0][None]], axis=0)
    behind = jnp.concatenate([before[0][None], field[:-1]], axis=0)
    advect = 0.5 * (ahead_x - behind_x)
    advect = advect + 0.5 * (wall_plus(flux_y) - wall_minus(flux_y))
    advect = advect + 0.5 * (jnp.roll(flux_z, -1, axis=2) - jnp.roll(flux_z, 1, axis=2))
    beside = ahead + behind
    beside = beside + wall_plus(field) + wall_minus(field)
    beside = beside + jnp.roll(field, -1, axis=2) + jnp.roll(field, 1, axis=2)
    operator = advect + viscosity * (beside - 6.0 * field) - reaction * field
    forcing = operator + source[0]

    kept = field + pseudo_step * forcing
    walls = jnp.stack([pulse[0] * kept[:, 0, :], field[:, 0, :]]).reshape(2, -1)
    onehot = (actuator[:, :, None] == jnp.arange(NACT, dtype=jnp.int32)[None, None, :]).astype(
        jnp.float32
    )
    terms = jnp.dot(
        walls,
        onehot.reshape(-1, NACT),
        precision=lax.Precision.HIGHEST,
        preferred_element_type=jnp.float32,
    )
    terms = butterfly_sum(terms, "space")
    slices = jnp.transpose(terms.reshape(2, count, share), (1, 0, 2))
    slices = jnp.pad(slices, ((0, 0), (0, 0), (0, cz - share)))
    pulse_row = jnp.broadcast_to(pulse.reshape(1, 1, 1), (count, 1, cz))
    grad_rows = jnp.concatenate([slices, pulse_row, jnp.zeros((count, pad - 3, cz), jnp.float32)], axis=1)
    forcing, grad_rows = lax.optimization_barrier((forcing, grad_rows))

    outgoing = jnp.concatenate([derived.reshape(count, chunk, cz), grad_rows], axis=1)
    incoming = lax.all_to_all(outgoing, "tm", 0, 0, tiled=True)
    time_term = incoming[:, :chunk].reshape(nx, cy, cz)
    weights = jnp.dot(dmat, incoming[:, chunk + 2, 0], precision=lax.Precision.HIGHEST)
    parts = incoming[:, chunk, :share] - pseudo_step * omega_rate * weights[:, None] * incoming[:, chunk + 1, :share]
    gradient = jnp.sum(parts, axis=0) / total

    updated = field - pseudo_step * (time_term - forcing)
    return (updated[None], gradient)


def solution(mesh):
    in_specs = (
        P("tm", "space", None, None),
        P(None, "tm", "space", None, None),
        P("tm", "space", None, None),
        P("tm"),
        P("space", None),
    )
    out_specs = (P("tm", "space", None, None), P("tm"))
    return jax.shard_map(
        on_device, mesh=mesh, in_specs=in_specs, out_specs=out_specs, check_vma=False
    )
```

```python
import math

import jax
import jax.numpy as jnp
from jax import lax
from jax.experimental import pallas as pl
from jax.experimental.pallas import tpu as pltpu
from jax.sharding import PartitionSpec as P

NACT = 128


omega_rate = 0.25
pseudo_step = 0.2
viscosity = 0.2
reaction = 0.5


def spectral_matrix(count):
    steps = jnp.arange(count, dtype=jnp.int32)
    offset = steps[:, None] - steps[None, :]
    theta = math.pi * offset.astype(jnp.float32) / count
    parity = jnp.where(offset % 2 == 0, 1.0, -1.0).astype(jnp.float32)
    skipped = (offset == 0) | (jnp.abs(offset) == count // 2)
    safe_tan = jnp.where(skipped, jnp.float32(1.0), jnp.tan(theta))
    return jnp.where(skipped, jnp.float32(0.0), 0.5 * parity / safe_tan).astype(jnp.float32)


def wall_plus(field):
    zeros = jnp.zeros_like(field[:, :1])
    return jnp.concatenate([field[:, 1:], zeros], axis=1)


def wall_minus(field):
    zeros = jnp.zeros_like(field[:, :1])
    return jnp.concatenate([zeros, field[:, :-1]], axis=1)


def butterfly_sum(x, axis):
    groups = lax.axis_size(axis)
    bit = 1
    while bit < groups:
        x = x + lax.ppermute(x, axis, [(i, i ^ bit) for i in range(groups)])
        bit *= 2
    return x


def halo(ends, axis):
    count = lax.axis_size(axis)
    up = [(i, (i + 1) % count) for i in range(count)]
    down = [(j, i) for i, j in up]
    before = lax.ppermute(ends[1], axis, up)
    after = lax.ppermute(ends[0], axis, down)
    return before, after


def stencil_kernel(pulse_ref, field_ref, vel_ref, src_ref, before_ref, after_ref, forcing_ref, walls_ref):
    nx, cy, cz = field_ref.shape
    row = lax.broadcasted_iota(jnp.int32, (cy, cz), 0)

    def wall_up(a):
        return jnp.where(row == cy - 1, 0.0, pltpu.roll(a, cy - 1, 0))

    def wall_down(a):
        return jnp.where(row == 0, 0.0, pltpu.roll(a, 1, 0))

    def span_up(a):
        return pltpu.roll(a, cz - 1, 1)

    def span_down(a):
        return pltpu.roll(a, 1, 1)

    for x in range(nx):
        f = field_ref[x]
        if x + 1 < nx:
            ahead, ahead_x = field_ref[x + 1], vel_ref[0, x + 1] * field_ref[x + 1]
        else:
            ahead, ahead_x = after_ref[0], after_ref[1]
        if x > 0:
            behind, behind_x = field_ref[x - 1], vel_ref[0, x - 1] * field_ref[x - 1]
        else:
            behind, behind_x = before_ref[0], before_ref[1]
        flux_y = vel_ref[1, x] * f
        flux_z = vel_ref[2, x] * f
        advect = 0.5 * (ahead_x - behind_x)
        advect = advect + 0.5 * (wall_up(flux_y) - wall_down(flux_y))
        advect = advect + 0.5 * (span_up(flux_z) - span_down(flux_z))
        beside = ahead + behind
        beside = beside + wall_up(f) + wall_down(f)
        beside = beside + span_up(f) + span_down(f)
        operator = advect + viscosity * (beside - 6.0 * f) - reaction * f
        forcing = operator + src_ref[x]
        forcing_ref[x] = forcing
        walls_ref[0, x : x + 1, :] = pulse_ref[0] * (f[0:1] + pseudo_step * forcing[0:1])
        walls_ref[1, x : x + 1, :] = f[0:1]


def stencil(pulse, field, velocity, source, before, after):
    nx, cy, cz = field.shape
    vmem = pl.BlockSpec(memory_space=pltpu.VMEM)
    return pl.pallas_call(
        stencil_kernel,
        out_shape=(
            jax.ShapeDtypeStruct((nx, cy, cz), jnp.float32),
            jax.ShapeDtypeStruct((2, nx, cz), jnp.float32),
        ),
        in_specs=[pl.BlockSpec(memory_space=pltpu.SMEM)] + [vmem] * 5,
        out_specs=(vmem, vmem),
    )(pulse, field, velocity, source, before, after)


def update_kernel(dmat_ref, buf_ref, field_ref, forcing_ref, out_ref, grad_ref):
    count = buf_ref.shape[0]
    chunk = buf_ref.shape[1] - 8
    for k in range(count):
        rows = slice(k * chunk, (k + 1) * chunk)
        out_ref[rows, :] = field_ref[rows, :] - pseudo_step * (buf_ref[k, :chunk, :] - forcing_ref[rows, :])
    weights = jnp.zeros((count, buf_ref.shape[2]), jnp.float32)
    for i in range(count):
        weights = weights + dmat_ref[:, i : i + 1] * buf_ref[i, chunk + 2 : chunk + 3, :]
    kept = buf_ref[:, chunk, :]
    plain = buf_ref[:, chunk + 1, :]
    parts = kept - pseudo_step * omega_rate * weights * plain
    grad_ref[...] = jnp.sum(parts, axis=0, keepdims=True) / count


def update(dmat, incoming, field, forcing):
    rows, cz = field.shape
    vmem = pl.BlockSpec(memory_space=pltpu.VMEM)
    return pl.pallas_call(
        update_kernel,
        out_shape=(
            jax.ShapeDtypeStruct((rows, cz), jnp.float32),
            jax.ShapeDtypeStruct((1, cz), jnp.float32),
        ),
        in_specs=[vmem] * 4,
        out_specs=(vmem, vmem),
    )(dmat, incoming, field, forcing)


def on_device(adjoint, base_flow, source, pulse, actuator):
    count = lax.axis_size("tm")
    nt_loc, nx, cy, cz = adjoint.shape
    total = count * nt_loc
    chunk = nx * cy // count
    share = NACT // count
    pad = 8
    dmat = spectral_matrix(total)

    incoming = lax.all_to_all(adjoint.reshape(count, chunk, cz), "tm", 0, 0, tiled=True)
    derived = omega_rate * jnp.einsum(
        "ji,jp->ip", dmat, incoming.reshape(total, chunk * cz), precision=lax.Precision.HIGHEST
    )

    field = adjoint[0]
    velocity = base_flow[:, 0]
    ends = [jnp.stack([field[k], velocity[0, k] * field[k]]) for k in (0, nx - 1)]
    before, after = halo(ends, "space")
    forcing, walls = stencil(pulse, field, velocity, source[0], before, after)

    onehot = (actuator[:, :, None] == jnp.arange(NACT, dtype=jnp.int32)[None, None, :]).astype(
        jnp.float32
    )
    terms = jnp.dot(
        walls.reshape(2, -1),
        onehot.reshape(-1, NACT),
        precision=lax.Precision.HIGHEST,
        preferred_element_type=jnp.float32,
    )
    terms = butterfly_sum(terms, "space")
    slices = jnp.transpose(terms.reshape(2, count, share), (1, 0, 2))
    slices = jnp.pad(slices, ((0, 0), (0, 0), (0, cz - share)))
    pulse_row = jnp.broadcast_to(pulse.reshape(1, 1, 1), (count, 1, cz))
    grad_rows = jnp.concatenate([slices, pulse_row, jnp.zeros((count, pad - 3, cz), jnp.float32)], axis=1)
    forcing, grad_rows = lax.optimization_barrier((forcing, grad_rows))

    outgoing = jnp.concatenate([derived.reshape(count, chunk, cz), grad_rows], axis=1)
    incoming = lax.all_to_all(outgoing, "tm", 0, 0, tiled=True)
    updated, gradient = update(dmat, incoming, field.reshape(nx * cy, cz), forcing.reshape(nx * cy, cz))
    return (updated.reshape(1, nx, cy, cz), gradient[0, :share])


def solution(mesh):
    in_specs = (
        P("tm", "space", None, None),
        P(None, "tm", "space", None, None),
        P("tm", "space", None, None),
        P("tm"),
        P("space", None),
    )
    out_specs = (P("tm", "space", None, None), P("tm"))
    return jax.shard_map(
        on_device, mesh=mesh, in_specs=in_specs, out_specs=out_specs, check_vma=False
    )
```

```python
import math

import jax
import jax.numpy as jnp
from jax import lax
from jax.experimental import pallas as pl
from jax.experimental.pallas import tpu as pltpu
from jax.sharding import PartitionSpec as P

NACT = 128


omega_rate = 0.25
pseudo_step = 0.2
viscosity = 0.2
reaction = 0.5


def spectral_matrix(count):
    steps = jnp.arange(count, dtype=jnp.int32)
    offset = steps[:, None] - steps[None, :]
    theta = math.pi * offset.astype(jnp.float32) / count
    parity = jnp.where(offset % 2 == 0, 1.0, -1.0).astype(jnp.float32)
    skipped = (offset == 0) | (jnp.abs(offset) == count // 2)
    safe_tan = jnp.where(skipped, jnp.float32(1.0), jnp.tan(theta))
    return jnp.where(skipped, jnp.float32(0.0), 0.5 * parity / safe_tan).astype(jnp.float32)


def wall_plus(field):
    zeros = jnp.zeros_like(field[:, :1])
    return jnp.concatenate([field[:, 1:], zeros], axis=1)


def wall_minus(field):
    zeros = jnp.zeros_like(field[:, :1])
    return jnp.concatenate([zeros, field[:, :-1]], axis=1)


def butterfly_sum(x, axis):
    groups = lax.axis_size(axis)
    bit = 1
    while bit < groups:
        x = x + lax.ppermute(x, axis, [(i, i ^ bit) for i in range(groups)])
        bit *= 2
    return x


def halo(ends, axis):
    count = lax.axis_size(axis)
    if count == 2:
        swapped = lax.ppermute(ends, axis, [(0, 1), (1, 0)])
        return swapped[1], swapped[0]
    up = [(i, (i + 1) % count) for i in range(count)]
    down = [(j, i) for i, j in up]
    before = lax.ppermute(ends[1], axis, up)
    after = lax.ppermute(ends[0], axis, down)
    return before, after


def stencil_kernel(pulse_ref, field_ref, vel_ref, src_ref, before_ref, after_ref, forcing_ref, walls_ref):
    nx, cy, cz = field_ref.shape
    row = lax.broadcasted_iota(jnp.int32, (cy, cz), 0)

    def wall_up(a):
        return jnp.where(row == cy - 1, 0.0, pltpu.roll(a, cy - 1, 0))

    def wall_down(a):
        return jnp.where(row == 0, 0.0, pltpu.roll(a, 1, 0))

    def span_up(a):
        return pltpu.roll(a, cz - 1, 1)

    def span_down(a):
        return pltpu.roll(a, 1, 1)

    for x in range(nx):
        f = field_ref[x]
        if x + 1 < nx:
            ahead, ahead_x = field_ref[x + 1], vel_ref[0, x + 1] * field_ref[x + 1]
        else:
            ahead, ahead_x = after_ref[0], after_ref[1]
        if x > 0:
            behind, behind_x = field_ref[x - 1], vel_ref[0, x - 1] * field_ref[x - 1]
        else:
            behind, behind_x = before_ref[0], before_ref[1]
        flux_y = vel_ref[1, x] * f
        flux_z = vel_ref[2, x] * f
        advect = 0.5 * (ahead_x - behind_x)
        advect = advect + 0.5 * (wall_up(flux_y) - wall_down(flux_y))
        advect = advect + 0.5 * (span_up(flux_z) - span_down(flux_z))
        beside = ahead + behind
        beside = beside + wall_up(f) + wall_down(f)
        beside = beside + span_up(f) + span_down(f)
        operator = advect + viscosity * (beside - 6.0 * f) - reaction * f
        forcing = operator + src_ref[x]
        forcing_ref[x] = forcing
        walls_ref[0, x : x + 1, :] = pulse_ref[0] * (f[0:1] + pseudo_step * forcing[0:1])
        walls_ref[1, x : x + 1, :] = f[0:1]


def stencil(pulse, field, velocity, source, before, after):
    nx, cy, cz = field.shape
    vmem = pl.BlockSpec(memory_space=pltpu.VMEM)
    return pl.pallas_call(
        stencil_kernel,
        out_shape=(
            jax.ShapeDtypeStruct((nx, cy, cz), jnp.float32),
            jax.ShapeDtypeStruct((2, nx, cz), jnp.float32),
        ),
        in_specs=[pl.BlockSpec(memory_space=pltpu.SMEM)] + [vmem] * 5,
        out_specs=(vmem, vmem),
    )(pulse, field, velocity, source, before, after)


def on_device(adjoint, base_flow, source, pulse, actuator):
    count = lax.axis_size("tm")
    nt_loc, nx, cy, cz = adjoint.shape
    total = count * nt_loc
    chunk = nx * cy // count
    share = NACT // count
    pad = 8
    dmat = spectral_matrix(total)

    incoming = lax.all_to_all(adjoint.reshape(count, chunk, cz), "tm", 0, 0, tiled=True)
    derived = omega_rate * jnp.einsum(
        "ji,jp->ip", dmat, incoming.reshape(total, chunk * cz), precision=lax.Precision.HIGHEST
    )

    field = adjoint[0]
    velocity = base_flow[:, 0]
    ends = jnp.stack([jnp.stack([field[k], velocity[0, k] * field[k]]) for k in (0, nx - 1)])
    before, after = halo(ends, "space")
    forcing, walls = stencil(pulse, field, velocity, source[0], before, after)

    onehot = (actuator[:, :, None] == jnp.arange(NACT, dtype=jnp.int32)[None, None, :]).astype(
        jnp.float32
    )
    terms = jnp.dot(
        walls.reshape(2, -1),
        onehot.reshape(-1, NACT),
        precision=lax.Precision.HIGHEST,
        preferred_element_type=jnp.float32,
    )
    terms = butterfly_sum(terms, "space")
    slices = jnp.transpose(terms.reshape(2, count, share), (1, 0, 2))
    slices = jnp.pad(slices, ((0, 0), (0, 0), (0, cz - share)))
    pulse_row = jnp.broadcast_to(pulse.reshape(1, 1, 1), (count, 1, cz))
    grad_rows = jnp.concatenate([slices, pulse_row, jnp.zeros((count, pad - 3, cz), jnp.float32)], axis=1)
    forcing, grad_rows = lax.optimization_barrier((forcing, grad_rows))

    outgoing = jnp.concatenate([derived.reshape(count, chunk, cz), grad_rows], axis=1)
    incoming = lax.all_to_all(outgoing, "tm", 0, 0, tiled=True)
    time_term = incoming[:, :chunk].reshape(nx, cy, cz)
    weights = jnp.dot(dmat, incoming[:, chunk + 2, 0], precision=lax.Precision.HIGHEST)
    parts = incoming[:, chunk, :share] - pseudo_step * omega_rate * weights[:, None] * incoming[:, chunk + 1, :share]
    gradient = jnp.sum(parts, axis=0) / total
    updated = field - pseudo_step * (time_term - forcing)
    return (updated[None], gradient)


def solution(mesh):
    in_specs = (
        P("tm", "space", None, None),
        P(None, "tm", "space", None, None),
        P("tm", "space", None, None),
        P("tm"),
        P("space", None),
    )
    out_specs = (P("tm", "space", None, None), P("tm"))
    return jax.shard_map(
        on_device, mesh=mesh, in_specs=in_specs, out_specs=out_specs, check_vma=False
    )
```

```python
import math

import jax
import jax.numpy as jnp
from jax import lax
from jax.experimental import pallas as pl
from jax.experimental.pallas import tpu as pltpu
from jax.sharding import PartitionSpec as P

NACT = 128


omega_rate = 0.25
pseudo_step = 0.2
viscosity = 0.2
reaction = 0.5


def spectral_matrix(count):
    steps = jnp.arange(count, dtype=jnp.int32)
    offset = steps[:, None] - steps[None, :]
    theta = math.pi * offset.astype(jnp.float32) / count
    parity = jnp.where(offset % 2 == 0, 1.0, -1.0).astype(jnp.float32)
    skipped = (offset == 0) | (jnp.abs(offset) == count // 2)
    safe_tan = jnp.where(skipped, jnp.float32(1.0), jnp.tan(theta))
    return jnp.where(skipped, jnp.float32(0.0), 0.5 * parity / safe_tan).astype(jnp.float32)


def wall_plus(field):
    zeros = jnp.zeros_like(field[:, :1])
    return jnp.concatenate([field[:, 1:], zeros], axis=1)


def wall_minus(field):
    zeros = jnp.zeros_like(field[:, :1])
    return jnp.concatenate([zeros, field[:, :-1]], axis=1)


def butterfly_sum(x, axis):
    groups = lax.axis_size(axis)
    bit = 1
    while bit < groups:
        x = x + lax.ppermute(x, axis, [(i, i ^ bit) for i in range(groups)])
        bit *= 2
    return x


def neighbours(slab, axis):
    count = lax.axis_size(axis)
    up = [(i, (i + 1) % count) for i in range(count)]
    down = [(j, i) for i, j in up]
    prev = lax.ppermute(slab, axis, up)
    if count == 2:
        return prev, prev
    return prev, lax.ppermute(slab, axis, down)


def stencil_kernel(pulse_ref, field_ref, vel_ref, src_ref, prev_ref, prev_u_ref, next_ref, next_u_ref, kept_ref, walls_ref):
    nx, cy, cz = field_ref.shape
    row = lax.broadcasted_iota(jnp.int32, (cy, cz), 0)

    def wall_up(a):
        return jnp.where(row == cy - 1, 0.0, pltpu.roll(a, cy - 1, 0))

    def wall_down(a):
        return jnp.where(row == 0, 0.0, pltpu.roll(a, 1, 0))

    def span_up(a):
        return pltpu.roll(a, cz - 1, 1)

    def span_down(a):
        return pltpu.roll(a, 1, 1)

    for x in range(nx):
        f = field_ref[x]
        if x + 1 < nx:
            ahead, ahead_x = field_ref[x + 1], vel_ref[0, x + 1] * field_ref[x + 1]
        else:
            ahead, ahead_x = next_ref[0, 0], next_u_ref[0, 0] * next_ref[0, 0]
        if x > 0:
            behind, behind_x = field_ref[x - 1], vel_ref[0, x - 1] * field_ref[x - 1]
        else:
            behind, behind_x = prev_ref[0, nx - 1], prev_u_ref[0, nx - 1] * prev_ref[0, nx - 1]
        flux_y = vel_ref[1, x] * f
        flux_z = vel_ref[2, x] * f
        advect = 0.5 * (ahead_x - behind_x)
        advect = advect + 0.5 * (wall_up(flux_y) - wall_down(flux_y))
        advect = advect + 0.5 * (span_up(flux_z) - span_down(flux_z))
        beside = ahead + behind
        beside = beside + wall_up(f) + wall_down(f)
        beside = beside + span_up(f) + span_down(f)
        operator = advect + viscosity * (beside - 6.0 * f) - reaction * f
        kept = f + pseudo_step * (operator + src_ref[x])
        kept_ref[x] = kept
        walls_ref[0, x : x + 1, :] = pulse_ref[0] * kept[0:1]
        walls_ref[1, x : x + 1, :] = f[0:1]


def stencil(pulse, field, velocity, source, prev, nxt):
    nx, cy, cz = field.shape
    vmem = pl.BlockSpec(memory_space=pltpu.VMEM)
    return pl.pallas_call(
        stencil_kernel,
        out_shape=(
            jax.ShapeDtypeStruct((nx, cy, cz), jnp.float32),
            jax.ShapeDtypeStruct((2, nx, cz), jnp.float32),
        ),
        in_specs=[pl.BlockSpec(memory_space=pltpu.SMEM)] + [vmem] * 7,
        out_specs=(vmem, vmem),
    )(pulse, field, velocity, source, *prev, *nxt)


def on_device(adjoint, base_flow, source, pulse, actuator):
    count = lax.axis_size("tm")
    nt_loc, nx, cy, cz = adjoint.shape
    total = count * nt_loc
    chunk = nx * cy // count
    share = NACT // count
    pad = 8
    dmat = spectral_matrix(total)

    incoming = lax.all_to_all(adjoint.reshape(count, chunk, cz), "tm", 0, 0, tiled=True)
    derived = omega_rate * jnp.einsum(
        "ji,jp->ip", dmat, incoming.reshape(total, chunk * cz), precision=lax.Precision.HIGHEST
    )

    field = adjoint[0]
    velocity = base_flow[:, 0]
    prev, nxt = neighbours((adjoint, base_flow[0]), "space")
    kept, walls = stencil(pulse, field, velocity, source[0], prev, nxt)

    onehot = (actuator[:, :, None] == jnp.arange(NACT, dtype=jnp.int32)[None, None, :]).astype(
        jnp.float32
    )
    terms = jnp.dot(
        walls.reshape(2, -1),
        onehot.reshape(-1, NACT),
        precision=lax.Precision.HIGHEST,
        preferred_element_type=jnp.float32,
    )
    terms = butterfly_sum(terms, "space")
    slices = jnp.transpose(terms.reshape(2, count, share), (1, 0, 2))
    slices = jnp.pad(slices, ((0, 0), (0, 0), (0, cz - share)))
    pulse_row = jnp.broadcast_to(pulse.reshape(1, 1, 1), (count, 1, cz))
    grad_rows = jnp.concatenate([slices, pulse_row, jnp.zeros((count, pad - 3, cz), jnp.float32)], axis=1)
    kept, grad_rows = lax.optimization_barrier((kept, grad_rows))

    outgoing = jnp.concatenate([derived.reshape(count, chunk, cz), grad_rows], axis=1)
    incoming = lax.all_to_all(outgoing, "tm", 0, 0, tiled=True)
    time_term = incoming[:, :chunk].reshape(nx, cy, cz)
    weights = jnp.dot(dmat, incoming[:, chunk + 2, 0], precision=lax.Precision.HIGHEST)
    parts = incoming[:, chunk, :share] - pseudo_step * omega_rate * weights[:, None] * incoming[:, chunk + 1, :share]
    gradient = jnp.sum(parts, axis=0) / total
    updated = kept - pseudo_step * time_term
    return (updated[None], gradient)


def solution(mesh):
    in_specs = (
        P("tm", "space", None, None),
        P(None, "tm", "space", None, None),
        P("tm", "space", None, None),
        P("tm"),
        P("space", None),
    )
    out_specs = (P("tm", "space", None, None), P("tm"))
    return jax.shard_map(
        on_device, mesh=mesh, in_specs=in_specs, out_specs=out_specs, check_vma=False
    )
```

```python
import math

import jax
import jax.numpy as jnp
from jax import lax
from jax.experimental import pallas as pl
from jax.experimental.pallas import tpu as pltpu
from jax.sharding import PartitionSpec as P

NACT = 128


omega_rate = 0.25
pseudo_step = 0.2
viscosity = 0.2
reaction = 0.5


def spectral_matrix(count):
    steps = jnp.arange(count, dtype=jnp.int32)
    offset = steps[:, None] - steps[None, :]
    theta = math.pi * offset.astype(jnp.float32) / count
    parity = jnp.where(offset % 2 == 0, 1.0, -1.0).astype(jnp.float32)
    skipped = (offset == 0) | (jnp.abs(offset) == count // 2)
    safe_tan = jnp.where(skipped, jnp.float32(1.0), jnp.tan(theta))
    return jnp.where(skipped, jnp.float32(0.0), 0.5 * parity / safe_tan).astype(jnp.float32)


def wall_plus(field):
    zeros = jnp.zeros_like(field[:, :1])
    return jnp.concatenate([field[:, 1:], zeros], axis=1)


def wall_minus(field):
    zeros = jnp.zeros_like(field[:, :1])
    return jnp.concatenate([zeros, field[:, :-1]], axis=1)


def butterfly_sum(x, axis):
    groups = lax.axis_size(axis)
    bit = 1
    while bit < groups:
        x = x + lax.ppermute(x, axis, [(i, i ^ bit) for i in range(groups)])
        bit *= 2
    return x


def neighbours(slab, axis):
    count = lax.axis_size(axis)
    up = [(i, (i + 1) % count) for i in range(count)]
    down = [(j, i) for i, j in up]
    prev = lax.ppermute(slab, axis, up)
    if count == 2:
        return prev, prev
    return prev, lax.ppermute(slab, axis, down)


def stencil_kernel(pulse_ref, field_ref, vel_ref, src_ref, prev_ref, prev_u_ref, next_ref, next_u_ref, kept_ref, walls_ref):
    nx, cy, cz = field_ref.shape
    row = lax.broadcasted_iota(jnp.int32, (cy, cz), 0)

    def wall_up(a):
        return jnp.where(row == cy - 1, 0.0, pltpu.roll(a, cy - 1, 0))

    def wall_down(a):
        return jnp.where(row == 0, 0.0, pltpu.roll(a, 1, 0))

    def span_up(a):
        return pltpu.roll(a, cz - 1, 1)

    def span_down(a):
        return pltpu.roll(a, 1, 1)

    for x in range(nx):
        f = field_ref[x]
        if x + 1 < nx:
            ahead, ahead_x = field_ref[x + 1], vel_ref[0, x + 1] * field_ref[x + 1]
        else:
            ahead, ahead_x = next_ref[0, 0], next_u_ref[0, 0] * next_ref[0, 0]
        if x > 0:
            behind, behind_x = field_ref[x - 1], vel_ref[0, x - 1] * field_ref[x - 1]
        else:
            behind, behind_x = prev_ref[0, nx - 1], prev_u_ref[0, nx - 1] * prev_ref[0, nx - 1]
        flux_y = vel_ref[1, x] * f
        flux_z = vel_ref[2, x] * f
        advect = 0.5 * (ahead_x - behind_x)
        advect = advect + 0.5 * (wall_up(flux_y) - wall_down(flux_y))
        advect = advect + 0.5 * (span_up(flux_z) - span_down(flux_z))
        beside = ahead + behind
        beside = beside + wall_up(f) + wall_down(f)
        beside = beside + span_up(f) + span_down(f)
        operator = advect + viscosity * (beside - 6.0 * f) - reaction * f
        kept = f + pseudo_step * (operator + src_ref[x])
        kept_ref[x] = kept
        walls_ref[0, x : x + 1, :] = pulse_ref[0] * kept[0:1]
        walls_ref[1, x : x + 1, :] = f[0:1]


def stencil(pulse, field, velocity, source, prev, nxt):
    nx, cy, cz = field.shape
    vmem = pl.BlockSpec(memory_space=pltpu.VMEM)
    return pl.pallas_call(
        stencil_kernel,
        out_shape=(
            jax.ShapeDtypeStruct((nx, cy, cz), jnp.float32),
            jax.ShapeDtypeStruct((2, nx, cz), jnp.float32),
        ),
        in_specs=[pl.BlockSpec(memory_space=pltpu.SMEM)] + [vmem] * 7,
        out_specs=(vmem, vmem),
    )(pulse, field, velocity, source, *prev, *nxt)


def on_device(adjoint, base_flow, source, pulse, actuator):
    count = lax.axis_size("tm")
    nt_loc, nx, cy, cz = adjoint.shape
    total = count * nt_loc
    chunk = nx * cy // count
    share = NACT // count
    pad = 8
    dmat = spectral_matrix(total)

    incoming = lax.all_to_all(adjoint.reshape(count, chunk, cz), "tm", 0, 0, tiled=True)
    derived = jnp.einsum(
        "ji,jp->ip",
        (-pseudo_step * omega_rate) * dmat,
        incoming.reshape(total, chunk * cz),
        precision=lax.Precision.HIGHEST,
    )

    field = adjoint[0]
    velocity = base_flow[:, 0]
    prev, nxt = neighbours((adjoint, base_flow[0]), "space")
    kept, walls = stencil(pulse, field, velocity, source[0], prev, nxt)

    onehot = (actuator[:, :, None] == jnp.arange(NACT, dtype=jnp.int32)[None, None, :]).astype(
        jnp.float32
    )
    terms = jnp.dot(
        walls.reshape(2, -1),
        onehot.reshape(-1, NACT),
        precision=lax.Precision.HIGHEST,
        preferred_element_type=jnp.float32,
    )
    terms = butterfly_sum(terms, "space")
    slices = jnp.transpose(terms.reshape(2, count, share), (1, 0, 2))
    slices = jnp.pad(slices, ((0, 0), (0, 0), (0, cz - share)))
    pulse_row = jnp.broadcast_to(pulse.reshape(1, 1, 1), (count, 1, cz))
    grad_rows = jnp.concatenate([slices, pulse_row, jnp.zeros((count, pad - 3, cz), jnp.float32)], axis=1)
    kept, grad_rows = lax.optimization_barrier((kept, grad_rows))

    outgoing = jnp.concatenate([derived.reshape(count, chunk, cz), grad_rows], axis=1)
    incoming = lax.all_to_all(outgoing, "tm", 0, 0, tiled=True)
    scaled_term = incoming[:, :chunk].reshape(nx, cy, cz)
    tile = incoming[:, chunk : chunk + 3, :share]
    weights = jnp.sum(dmat * tile[None, :, 2, 0], axis=1)
    parts = tile[:, 0] - pseudo_step * omega_rate * weights[:, None] * tile[:, 1]
    gradient = jnp.sum(parts, axis=0) / total
    updated = kept + scaled_term
    return (updated[None], gradient)


def solution(mesh):
    in_specs = (
        P("tm", "space", None, None),
        P(None, "tm", "space", None, None),
        P("tm", "space", None, None),
        P("tm"),
        P("space", None),
    )
    out_specs = (P("tm", "space", None, None), P("tm"))
    return jax.shard_map(
        on_device, mesh=mesh, in_specs=in_specs, out_specs=out_specs, check_vma=False
    )
```

```python
import math

import jax
import jax.numpy as jnp
from jax import lax
from jax.experimental import pallas as pl
from jax.experimental.pallas import tpu as pltpu
from jax.sharding import PartitionSpec as P

NACT = 128


omega_rate = 0.25
pseudo_step = 0.2
viscosity = 0.2
reaction = 0.5


def spectral_matrix(count):
    steps = jnp.arange(count, dtype=jnp.int32)
    offset = steps[:, None] - steps[None, :]
    theta = math.pi * offset.astype(jnp.float32) / count
    parity = jnp.where(offset % 2 == 0, 1.0, -1.0).astype(jnp.float32)
    skipped = (offset == 0) | (jnp.abs(offset) == count // 2)
    safe_tan = jnp.where(skipped, jnp.float32(1.0), jnp.tan(theta))
    return jnp.where(skipped, jnp.float32(0.0), 0.5 * parity / safe_tan).astype(jnp.float32)


def wall_plus(field):
    zeros = jnp.zeros_like(field[:, :1])
    return jnp.concatenate([field[:, 1:], zeros], axis=1)


def wall_minus(field):
    zeros = jnp.zeros_like(field[:, :1])
    return jnp.concatenate([zeros, field[:, :-1]], axis=1)


def butterfly_sum(x, axis):
    groups = lax.axis_size(axis)
    bit = 1
    while bit < groups:
        x = x + lax.ppermute(x, axis, [(i, i ^ bit) for i in range(groups)])
        bit *= 2
    return x


def neighbours(slab, axis):
    count = lax.axis_size(axis)
    up = [(i, (i + 1) % count) for i in range(count)]
    down = [(j, i) for i, j in up]
    prev = lax.ppermute(slab, axis, up)
    if count == 2:
        return prev, prev
    return prev, lax.ppermute(slab, axis, down)


def stencil_kernel(pulse_ref, field_ref, vel_ref, src_ref, prev_ref, prev_u_ref, next_ref, next_u_ref, kept_ref, walls_ref):
    nx, cy, cz = field_ref.shape
    row = lax.broadcasted_iota(jnp.int32, (cy, cz), 0)

    def wall_up(a):
        return jnp.where(row == cy - 1, 0.0, pltpu.roll(a, cy - 1, 0))

    def wall_down(a):
        return jnp.where(row == 0, 0.0, pltpu.roll(a, 1, 0))

    def span_up(a):
        return pltpu.roll(a, cz - 1, 1)

    def span_down(a):
        return pltpu.roll(a, 1, 1)

    for x in range(nx):
        f = field_ref[x]
        if x + 1 < nx:
            ahead, ahead_x = field_ref[x + 1], vel_ref[0, x + 1] * field_ref[x + 1]
        else:
            ahead, ahead_x = next_ref[0, 0], next_u_ref[0, 0, 0] * next_ref[0, 0]
        if x > 0:
            behind, behind_x = field_ref[x - 1], vel_ref[0, x - 1] * field_ref[x - 1]
        else:
            behind, behind_x = prev_ref[0, nx - 1], prev_u_ref[0, 0, nx - 1] * prev_ref[0, nx - 1]
        flux_y = vel_ref[1, x] * f
        flux_z = vel_ref[2, x] * f
        advect = 0.5 * (ahead_x - behind_x)
        advect = advect + 0.5 * (wall_up(flux_y) - wall_down(flux_y))
        advect = advect + 0.5 * (span_up(flux_z) - span_down(flux_z))
        beside = ahead + behind
        beside = beside + wall_up(f) + wall_down(f)
        beside = beside + span_up(f) + span_down(f)
        operator = advect + viscosity * (beside - 6.0 * f) - reaction * f
        kept = f + pseudo_step * (operator + src_ref[x])
        kept_ref[x] = kept
        walls_ref[0, x : x + 1, :] = pulse_ref[0] * kept[0:1]
        walls_ref[1, x : x + 1, :] = f[0:1]


def stencil(pulse, field, velocity, source, prev, nxt):
    nx, cy, cz = field.shape
    vmem = pl.BlockSpec(memory_space=pltpu.VMEM)
    return pl.pallas_call(
        stencil_kernel,
        out_shape=(
            jax.ShapeDtypeStruct((nx, cy, cz), jnp.float32),
            jax.ShapeDtypeStruct((2, nx, cz), jnp.float32),
        ),
        in_specs=[pl.BlockSpec(memory_space=pltpu.SMEM)] + [vmem] * 7,
        out_specs=(vmem, vmem),
    )(pulse, field, velocity, source, *prev, *nxt)


def on_device(adjoint, base_flow, source, pulse, actuator):
    count = lax.axis_size("tm")
    nt_loc, nx, cy, cz = adjoint.shape
    total = count * nt_loc
    chunk = nx * cy // count
    share = NACT // count
    pad = 8
    dmat = spectral_matrix(total)

    incoming = lax.all_to_all(adjoint.reshape(count, chunk, cz), "tm", 0, 0, tiled=True)
    derived = jnp.einsum(
        "ji,jp->ip",
        (-pseudo_step * omega_rate) * dmat,
        incoming.reshape(total, chunk * cz),
        precision=lax.Precision.HIGHEST,
    )

    field = adjoint[0]
    velocity = base_flow[:, 0]
    prev, nxt = neighbours((adjoint, base_flow), "space")
    kept, walls = stencil(pulse, field, velocity, source[0], prev, nxt)

    onehot = (actuator[:, :, None] == jnp.arange(NACT, dtype=jnp.int32)[None, None, :]).astype(
        jnp.float32
    )
    terms = jnp.dot(
        walls.reshape(2, -1),
        onehot.reshape(-1, NACT),
        precision=lax.Precision.HIGHEST,
        preferred_element_type=jnp.float32,
    )
    terms = butterfly_sum(terms, "space")
    slices = jnp.transpose(terms.reshape(2, count, share), (1, 0, 2))
    slices = jnp.pad(slices, ((0, 0), (0, 0), (0, cz - share)))
    pulse_row = jnp.broadcast_to(pulse.reshape(1, 1, 1), (count, 1, cz))
    grad_rows = jnp.concatenate([slices, pulse_row, jnp.zeros((count, pad - 3, cz), jnp.float32)], axis=1)
    kept, grad_rows = lax.optimization_barrier((kept, grad_rows))

    outgoing = jnp.concatenate([derived.reshape(count, chunk, cz), grad_rows], axis=1)
    incoming = lax.all_to_all(outgoing, "tm", 0, 0, tiled=True)
    scaled_term = incoming[:, :chunk].reshape(nx, cy, cz)
    tile = incoming[:, chunk : chunk + 3, :share]
    weights = jnp.sum(dmat * tile[None, :, 2, 0], axis=1)
    parts = tile[:, 0] - pseudo_step * omega_rate * weights[:, None] * tile[:, 1]
    gradient = jnp.sum(parts, axis=0) / total
    updated = kept + scaled_term
    return (updated[None], gradient)


def solution(mesh):
    in_specs = (
        P("tm", "space", None, None),
        P(None, "tm", "space", None, None),
        P("tm", "space", None, None),
        P("tm"),
        P("space", None),
    )
    out_specs = (P("tm", "space", None, None), P("tm"))
    return jax.shard_map(
        on_device, mesh=mesh, in_specs=in_specs, out_specs=out_specs, check_vma=False
    )
```

```python
import math

import jax
import jax.numpy as jnp
from jax import lax
from jax.experimental import pallas as pl
from jax.experimental.pallas import tpu as pltpu
from jax.sharding import PartitionSpec as P

NACT = 128


omega_rate = 0.25
pseudo_step = 0.2
viscosity = 0.2
reaction = 0.5


def spectral_matrix(count):
    steps = jnp.arange(count, dtype=jnp.int32)
    offset = steps[:, None] - steps[None, :]
    theta = math.pi * offset.astype(jnp.float32) / count
    parity = jnp.where(offset % 2 == 0, 1.0, -1.0).astype(jnp.float32)
    skipped = (offset == 0) | (jnp.abs(offset) == count // 2)
    safe_tan = jnp.where(skipped, jnp.float32(1.0), jnp.tan(theta))
    return jnp.where(skipped, jnp.float32(0.0), 0.5 * parity / safe_tan).astype(jnp.float32)


def wall_plus(field):
    zeros = jnp.zeros_like(field[:, :1])
    return jnp.concatenate([field[:, 1:], zeros], axis=1)


def wall_minus(field):
    zeros = jnp.zeros_like(field[:, :1])
    return jnp.concatenate([zeros, field[:, :-1]], axis=1)


def butterfly_sum(x, axis):
    groups = lax.axis_size(axis)
    bit = 1
    while bit < groups:
        x = x + lax.ppermute(x, axis, [(i, i ^ bit) for i in range(groups)])
        bit *= 2
    return x


def neighbours(slab, axis):
    count = lax.axis_size(axis)
    up = [(i, (i + 1) % count) for i in range(count)]
    down = [(j, i) for i, j in up]
    prev = lax.ppermute(slab, axis, up)
    if count == 2:
        return prev, prev
    return prev, lax.ppermute(slab, axis, down)


def stencil_kernel(pulse_ref, field_ref, vel_ref, src_ref, prev_ref, prev_u_ref, next_ref, next_u_ref, kept_ref, walls_ref):
    nx, cy, cz = field_ref.shape
    row = lax.broadcasted_iota(jnp.int32, (cy, cz), 0)

    def wall_up(a):
        return jnp.where(row == cy - 1, 0.0, pltpu.roll(a, cy - 1, 0))

    def wall_down(a):
        return jnp.where(row == 0, 0.0, pltpu.roll(a, 1, 0))

    def span_up(a):
        return pltpu.roll(a, cz - 1, 1)

    def span_down(a):
        return pltpu.roll(a, 1, 1)

    for x in range(nx):
        f = field_ref[x]
        if x + 1 < nx:
            ahead, ahead_x = field_ref[x + 1], vel_ref[0, x + 1] * field_ref[x + 1]
        else:
            ahead, ahead_x = next_ref[0, 0], next_u_ref[0, 0, 0] * next_ref[0, 0]
        if x > 0:
            behind, behind_x = field_ref[x - 1], vel_ref[0, x - 1] * field_ref[x - 1]
        else:
            behind, behind_x = prev_ref[0, nx - 1], prev_u_ref[0, 0, nx - 1] * prev_ref[0, nx - 1]
        flux_y = vel_ref[1, x] * f
        flux_z = vel_ref[2, x] * f
        advect = 0.5 * (ahead_x - behind_x)
        advect = advect + 0.5 * (wall_up(flux_y) - wall_down(flux_y))
        advect = advect + 0.5 * (span_up(flux_z) - span_down(flux_z))
        beside = ahead + behind
        beside = beside + wall_up(f) + wall_down(f)
        beside = beside + span_up(f) + span_down(f)
        operator = advect + viscosity * (beside - 6.0 * f) - reaction * f
        kept = f + pseudo_step * (operator + src_ref[x])
        kept_ref[x] = kept
        walls_ref[0, x : x + 1, :] = pulse_ref[0] * kept[0:1]
        walls_ref[1, x : x + 1, :] = f[0:1]


def stencil(pulse, field, velocity, source, prev, nxt):
    nx, cy, cz = field.shape
    vmem = pl.BlockSpec(memory_space=pltpu.VMEM)
    return pl.pallas_call(
        stencil_kernel,
        out_shape=(
            jax.ShapeDtypeStruct((nx, cy, cz), jnp.float32),
            jax.ShapeDtypeStruct((2, nx, cz), jnp.float32),
        ),
        in_specs=[pl.BlockSpec(memory_space=pltpu.SMEM)] + [vmem] * 7,
        out_specs=(vmem, vmem),
    )(pulse, field, velocity, source, *prev, *nxt)


def on_device(adjoint, base_flow, source, pulse, actuator):
    count = lax.axis_size("tm")
    nt_loc, nx, cy, cz = adjoint.shape
    total = count * nt_loc
    chunk = nx * cy // count
    share = NACT // count
    pad = 8
    dmat = spectral_matrix(total)

    incoming = lax.all_to_all(adjoint.reshape(count, chunk, cz), "tm", 0, 0, tiled=True)
    derived = jnp.einsum(
        "ji,jp->ip",
        (-pseudo_step * omega_rate) * dmat,
        incoming.reshape(total, chunk * cz),
        precision=lax.Precision.HIGHEST,
    )

    field = adjoint[0]
    velocity = base_flow[:, 0]
    prev, nxt = neighbours((adjoint, base_flow), "space")
    kept, walls = stencil(pulse, field, velocity, source[0], prev, nxt)

    onehot = (actuator[:, :, None] == jnp.arange(NACT, dtype=jnp.int32)[None, None, :]).astype(
        jnp.float32
    )
    terms = jnp.dot(
        walls.reshape(2, -1),
        onehot.reshape(-1, NACT),
        precision=lax.Precision.HIGHEST,
        preferred_element_type=jnp.float32,
    )
    terms = butterfly_sum(terms, "space")
    scales = jnp.array([1.0, -pseudo_step * omega_rate], jnp.float32)[:, None] / total
    slices = jnp.transpose((terms * scales).reshape(2, count, share), (1, 0, 2))
    slices = jnp.pad(slices, ((0, 0), (0, 0), (0, cz - share)))
    pulse_row = jnp.broadcast_to(pulse.reshape(1, 1, 1), (count, 1, cz))
    grad_rows = jnp.concatenate([slices, pulse_row, jnp.zeros((count, pad - 3, cz), jnp.float32)], axis=1)
    kept, grad_rows = lax.optimization_barrier((kept, grad_rows))

    outgoing = jnp.concatenate([derived.reshape(count, chunk, cz), grad_rows], axis=1)
    incoming = lax.all_to_all(outgoing, "tm", 0, 0, tiled=True)
    scaled_term = incoming[:, :chunk].reshape(nx, cy, cz)
    tile = incoming[:, chunk : chunk + 3, :share]
    weights = jnp.sum(dmat * tile[None, :, 2, 0], axis=1)
    gradient = jnp.sum(tile[:, 0] + weights[:, None] * tile[:, 1], axis=0)
    updated = kept + scaled_term
    return (updated[None], gradient)


def solution(mesh):
    in_specs = (
        P("tm", "space", None, None),
        P(None, "tm", "space", None, None),
        P("tm", "space", None, None),
        P("tm"),
        P("space", None),
    )
    out_specs = (P("tm", "space", None, None), P("tm"))
    return jax.shard_map(
        on_device, mesh=mesh, in_specs=in_specs, out_specs=out_specs, check_vma=False
    )
```

```python
import math

import jax
import jax.numpy as jnp
from jax import lax
from jax.experimental import pallas as pl
from jax.experimental.pallas import tpu as pltpu
from jax.sharding import PartitionSpec as P

NACT = 128


omega_rate = 0.25
pseudo_step = 0.2
viscosity = 0.2
reaction = 0.5


def spectral_matrix(count):
    steps = jnp.arange(count, dtype=jnp.int32)
    offset = steps[:, None] - steps[None, :]
    theta = math.pi * offset.astype(jnp.float32) / count
    parity = jnp.where(offset % 2 == 0, 1.0, -1.0).astype(jnp.float32)
    skipped = (offset == 0) | (jnp.abs(offset) == count // 2)
    safe_tan = jnp.where(skipped, jnp.float32(1.0), jnp.tan(theta))
    return jnp.where(skipped, jnp.float32(0.0), 0.5 * parity / safe_tan).astype(jnp.float32)


def wall_plus(field):
    zeros = jnp.zeros_like(field[:, :1])
    return jnp.concatenate([field[:, 1:], zeros], axis=1)


def wall_minus(field):
    zeros = jnp.zeros_like(field[:, :1])
    return jnp.concatenate([zeros, field[:, :-1]], axis=1)


def butterfly_sum(x, axis):
    groups = lax.axis_size(axis)
    bit = 1
    while bit < groups:
        x = x + lax.ppermute(x, axis, [(i, i ^ bit) for i in range(groups)])
        bit *= 2
    return x


def neighbours(slab, axis):
    count = lax.axis_size(axis)
    up = [(i, (i + 1) % count) for i in range(count)]
    down = [(j, i) for i, j in up]
    prev = lax.ppermute(slab, axis, up)
    if count == 2:
        return prev, prev
    return prev, lax.ppermute(slab, axis, down)


def kept_layers(pulse_ref, field_ref, vel_ref, src_ref, prev_ref, prev_u_ref, next_ref, next_u_ref):
    nx, cy, cz = field_ref.shape
    row = lax.broadcasted_iota(jnp.int32, (cy, cz), 0)

    def wall_up(a):
        return jnp.where(row == cy - 1, 0.0, pltpu.roll(a, cy - 1, 0))

    def wall_down(a):
        return jnp.where(row == 0, 0.0, pltpu.roll(a, 1, 0))

    def span_up(a):
        return pltpu.roll(a, cz - 1, 1)

    def span_down(a):
        return pltpu.roll(a, 1, 1)

    for x in range(nx):
        f = field_ref[x]
        if x + 1 < nx:
            ahead, ahead_x = field_ref[x + 1], vel_ref[0, x + 1] * field_ref[x + 1]
        else:
            ahead, ahead_x = next_ref[0, 0], next_u_ref[0, 0, 0] * next_ref[0, 0]
        if x > 0:
            behind, behind_x = field_ref[x - 1], vel_ref[0, x - 1] * field_ref[x - 1]
        else:
            behind, behind_x = prev_ref[0, nx - 1], prev_u_ref[0, 0, nx - 1] * prev_ref[0, nx - 1]
        flux_y = vel_ref[1, x] * f
        flux_z = vel_ref[2, x] * f
        advect = 0.5 * (ahead_x - behind_x)
        advect = advect + 0.5 * (wall_up(flux_y) - wall_down(flux_y))
        advect = advect + 0.5 * (span_up(flux_z) - span_down(flux_z))
        beside = ahead + behind
        beside = beside + wall_up(f) + wall_down(f)
        beside = beside + span_up(f) + span_down(f)
        operator = advect + viscosity * (beside - 6.0 * f) - reaction * f
        yield x, f, f + pseudo_step * (operator + src_ref[x])


def walls_kernel(*refs):
    *ins, walls_ref = refs
    pulse_ref = ins[0]
    for x, f, kept in kept_layers(*ins):
        walls_ref[0, x : x + 1, :] = pulse_ref[0] * kept[0:1]
        walls_ref[1, x : x + 1, :] = f[0:1]


def kept_kernel(*refs):
    *ins, _, kept_ref = refs
    for x, _, kept in kept_layers(*ins):
        kept_ref[x] = kept


def tile_spec(shape, rows):
    block = shape[:-2] + (rows, shape[-1])
    return pl.BlockSpec(block, lambda i: (0,) * len(shape))


def wall_terms(pulse, field, velocity, source, prev, nxt):
    nx, cy, cz = field.shape
    operands = (field, velocity, source, *prev, *nxt)
    return pl.pallas_call(
        walls_kernel,
        grid=(1,),
        out_shape=jax.ShapeDtypeStruct((2, nx, cz), jnp.float32),
        in_specs=[pl.BlockSpec(memory_space=pltpu.SMEM)] + [tile_spec(op.shape, 8) for op in operands],
        out_specs=pl.BlockSpec((2, nx, cz), lambda i: (0, 0, 0)),
    )(pulse, *operands)


def kept_field(pulse, field, velocity, source, prev, nxt, after):
    nx, cy, cz = field.shape
    vmem = pl.BlockSpec(memory_space=pltpu.VMEM)
    return pl.pallas_call(
        kept_kernel,
        out_shape=jax.ShapeDtypeStruct((nx, cy, cz), jnp.float32),
        in_specs=[pl.BlockSpec(memory_space=pltpu.SMEM)] + [vmem] * 7 + [pl.BlockSpec(memory_space=pl.ANY)],
        out_specs=vmem,
    )(pulse, field, velocity, source, *prev, *nxt, after)


def on_device(adjoint, base_flow, source, pulse, actuator):
    count = lax.axis_size("tm")
    nt_loc, nx, cy, cz = adjoint.shape
    total = count * nt_loc
    chunk = nx * cy // count
    share = NACT // count
    pad = 8
    dmat = spectral_matrix(total)

    incoming = lax.all_to_all(adjoint.reshape(count, chunk, cz), "tm", 0, 0, tiled=True)
    derived = jnp.einsum(
        "ji,jp->ip",
        (-pseudo_step * omega_rate) * dmat,
        incoming.reshape(total, chunk * cz),
        precision=lax.Precision.HIGHEST,
    )

    field = adjoint[0]
    velocity = base_flow[:, 0]
    prev, nxt = neighbours((adjoint, base_flow), "space")
    walls = wall_terms(pulse, field, velocity, source[0], prev, nxt)
    kept = kept_field(pulse, field, velocity, source[0], prev, nxt, incoming)

    onehot = (actuator[:, :, None] == jnp.arange(NACT, dtype=jnp.int32)[None, None, :]).astype(
        jnp.float32
    )
    terms = jnp.dot(
        walls.reshape(2, -1),
        onehot.reshape(-1, NACT),
        precision=lax.Precision.HIGHEST,
        preferred_element_type=jnp.float32,
    )
    terms = butterfly_sum(terms, "space")
    scales = jnp.array([1.0, -pseudo_step * omega_rate], jnp.float32)[:, None] / total
    slices = jnp.transpose((terms * scales).reshape(2, count, share), (1, 0, 2))
    slices = jnp.pad(slices, ((0, 0), (0, 0), (0, cz - share)))
    pulse_row = jnp.broadcast_to(pulse.reshape(1, 1, 1), (count, 1, cz))
    grad_rows = jnp.concatenate([slices, pulse_row, jnp.zeros((count, pad - 3, cz), jnp.float32)], axis=1)

    outgoing = jnp.concatenate([derived.reshape(count, chunk, cz), grad_rows], axis=1)
    incoming = lax.all_to_all(outgoing, "tm", 0, 0, tiled=True)
    scaled_term = incoming[:, :chunk].reshape(nx, cy, cz)
    tile = incoming[:, chunk : chunk + 3, :share]
    weights = jnp.sum(dmat * tile[None, :, 2, 0], axis=1)
    gradient = jnp.sum(tile[:, 0] + weights[:, None] * tile[:, 1], axis=0)
    updated = kept + scaled_term
    return (updated[None], gradient)


def solution(mesh):
    in_specs = (
        P("tm", "space", None, None),
        P(None, "tm", "space", None, None),
        P("tm", "space", None, None),
        P("tm"),
        P("space", None),
    )
    out_specs = (P("tm", "space", None, None), P("tm"))
    return jax.shard_map(
        on_device, mesh=mesh, in_specs=in_specs, out_specs=out_specs, check_vma=False
    )
```

```python
import math

import jax
import jax.numpy as jnp
from jax import lax
from jax.experimental import pallas as pl
from jax.experimental.pallas import tpu as pltpu
from jax.sharding import PartitionSpec as P

NACT = 128


omega_rate = 0.25
pseudo_step = 0.2
viscosity = 0.2
reaction = 0.5


def spectral_matrix(count):
    steps = jnp.arange(count, dtype=jnp.int32)
    offset = steps[:, None] - steps[None, :]
    theta = math.pi * offset.astype(jnp.float32) / count
    parity = jnp.where(offset % 2 == 0, 1.0, -1.0).astype(jnp.float32)
    skipped = (offset == 0) | (jnp.abs(offset) == count // 2)
    safe_tan = jnp.where(skipped, jnp.float32(1.0), jnp.tan(theta))
    return jnp.where(skipped, jnp.float32(0.0), 0.5 * parity / safe_tan).astype(jnp.float32)


def wall_plus(field):
    zeros = jnp.zeros_like(field[:, :1])
    return jnp.concatenate([field[:, 1:], zeros], axis=1)


def wall_minus(field):
    zeros = jnp.zeros_like(field[:, :1])
    return jnp.concatenate([zeros, field[:, :-1]], axis=1)


def butterfly_sum(x, axis):
    groups = lax.axis_size(axis)
    bit = 1
    while bit < groups:
        x = x + lax.ppermute(x, axis, [(i, i ^ bit) for i in range(groups)])
        bit *= 2
    return x


def neighbours(slab, axis):
    count = lax.axis_size(axis)
    up = [(i, (i + 1) % count) for i in range(count)]
    down = [(j, i) for i, j in up]
    prev = lax.ppermute(slab, axis, up)
    if count == 2:
        return prev, prev
    return prev, lax.ppermute(slab, axis, down)


def stencil_kernel(pulse_ref, field_ref, vel_ref, src_ref, prev_ref, prev_u_ref, next_ref, next_u_ref, kept_ref, walls_ref):
    nx, cy, cz = field_ref.shape
    row = lax.broadcasted_iota(jnp.int32, (cy, cz), 0)

    def wall_up(a):
        return jnp.where(row == cy - 1, 0.0, pltpu.roll(a, cy - 1, 0))

    def wall_down(a):
        return jnp.where(row == 0, 0.0, pltpu.roll(a, 1, 0))

    def span_up(a):
        return pltpu.roll(a, cz - 1, 1)

    def span_down(a):
        return pltpu.roll(a, 1, 1)

    for x in range(nx):
        f = field_ref[x]
        if x + 1 < nx:
            ahead, ahead_x = field_ref[x + 1], vel_ref[0, x + 1] * field_ref[x + 1]
        else:
            ahead, ahead_x = next_ref[0, 0], next_u_ref[0, 0, 0] * next_ref[0, 0]
        if x > 0:
            behind, behind_x = field_ref[x - 1], vel_ref[0, x - 1] * field_ref[x - 1]
        else:
            behind, behind_x = prev_ref[0, 0], prev_u_ref[0, 0, 0] * prev_ref[0, 0]
        flux_y = vel_ref[1, x] * f
        flux_z = vel_ref[2, x] * f
        advect = 0.5 * (ahead_x - behind_x)
        advect = advect + 0.5 * (wall_up(flux_y) - wall_down(flux_y))
        advect = advect + 0.5 * (span_up(flux_z) - span_down(flux_z))
        beside = ahead + behind
        beside = beside + wall_up(f) + wall_down(f)
        beside = beside + span_up(f) + span_down(f)
        operator = advect + viscosity * (beside - 6.0 * f) - reaction * f
        kept = f + pseudo_step * (operator + src_ref[x])
        kept_ref[x] = kept
        walls_ref[0, x : x + 1, :] = pulse_ref[0] * kept[0:1]
        walls_ref[1, x : x + 1, :] = f[0:1]


def whole(shape):
    return pl.BlockSpec(shape, lambda i: (0,) * len(shape))


def layer(shape, dim, at):
    block = tuple(1 if d == dim else n for d, n in enumerate(shape))
    return pl.BlockSpec(block, lambda i: tuple(at if d == dim else 0 for d in range(len(shape))))


def stencil(pulse, field, velocity, source, prev, nxt):
    nx, cy, cz = field.shape
    slab, flow = prev[0].shape, prev[1].shape
    return pl.pallas_call(
        stencil_kernel,
        grid=(1,),
        out_shape=(
            jax.ShapeDtypeStruct((nx, cy, cz), jnp.float32),
            jax.ShapeDtypeStruct((2, nx, cz), jnp.float32),
        ),
        in_specs=[
            pl.BlockSpec(memory_space=pltpu.SMEM),
            whole(field.shape),
            whole(velocity.shape),
            whole(source.shape),
            layer(slab, 1, nx - 1),
            layer(flow, 2, nx - 1),
            layer(slab, 1, 0),
            layer(flow, 2, 0),
        ],
        out_specs=(whole((nx, cy, cz)), whole((2, nx, cz))),
    )(pulse, field, velocity, source, *prev, *nxt)


def on_device(adjoint, base_flow, source, pulse, actuator):
    count = lax.axis_size("tm")
    nt_loc, nx, cy, cz = adjoint.shape
    total = count * nt_loc
    chunk = nx * cy // count
    share = NACT // count
    pad = 8
    dmat = spectral_matrix(total)

    incoming = lax.all_to_all(adjoint.reshape(count, chunk, cz), "tm", 0, 0, tiled=True)
    derived = jnp.einsum(
        "ji,jp->ip",
        (-pseudo_step * omega_rate) * dmat,
        incoming.reshape(total, chunk * cz),
        precision=lax.Precision.HIGHEST,
    )

    field = adjoint[0]
    velocity = base_flow[:, 0]
    prev, nxt = neighbours((adjoint, base_flow), "space")
    kept, walls = stencil(pulse, field, velocity, source[0], prev, nxt)

    onehot = (actuator[:, :, None] == jnp.arange(NACT, dtype=jnp.int32)[None, None, :]).astype(
        jnp.float32
    )
    terms = jnp.dot(
        walls.reshape(2, -1),
        onehot.reshape(-1, NACT),
        precision=lax.Precision.HIGHEST,
        preferred_element_type=jnp.float32,
    )
    terms = butterfly_sum(terms, "space")
    scales = jnp.array([1.0, -pseudo_step * omega_rate], jnp.float32)[:, None] / total
    slices = jnp.transpose((terms * scales).reshape(2, count, share), (1, 0, 2))
    slices = jnp.pad(slices, ((0, 0), (0, 0), (0, cz - share)))
    pulse_row = jnp.broadcast_to(pulse.reshape(1, 1, 1), (count, 1, cz))
    grad_rows = jnp.concatenate([slices, pulse_row, jnp.zeros((count, pad - 3, cz), jnp.float32)], axis=1)
    kept, grad_rows = lax.optimization_barrier((kept, grad_rows))

    outgoing = jnp.concatenate([derived.reshape(count, chunk, cz), grad_rows], axis=1)
    incoming = lax.all_to_all(outgoing, "tm", 0, 0, tiled=True)
    scaled_term = incoming[:, :chunk].reshape(nx, cy, cz)
    tile = incoming[:, chunk : chunk + 3, :share]
    weights = jnp.sum(dmat * tile[None, :, 2, 0], axis=1)
    gradient = jnp.sum(tile[:, 0] + weights[:, None] * tile[:, 1], axis=0)
    updated = kept + scaled_term
    return (updated[None], gradient)


def solution(mesh):
    in_specs = (
        P("tm", "space", None, None),
        P(None, "tm", "space", None, None),
        P("tm", "space", None, None),
        P("tm"),
        P("space", None),
    )
    out_specs = (P("tm", "space", None, None), P("tm"))
    return jax.shard_map(
        on_device, mesh=mesh, in_specs=in_specs, out_specs=out_specs, check_vma=False
    )
```

```python
import math

import jax
import jax.numpy as jnp
from jax import lax
from jax.experimental import pallas as pl
from jax.experimental.pallas import tpu as pltpu
from jax.sharding import PartitionSpec as P

NACT = 128


omega_rate = 0.25
pseudo_step = 0.2
viscosity = 0.2
reaction = 0.5


def spectral_matrix(count):
    steps = jnp.arange(count, dtype=jnp.int32)
    offset = steps[:, None] - steps[None, :]
    theta = math.pi * offset.astype(jnp.float32) / count
    parity = jnp.where(offset % 2 == 0, 1.0, -1.0).astype(jnp.float32)
    skipped = (offset == 0) | (jnp.abs(offset) == count // 2)
    safe_tan = jnp.where(skipped, jnp.float32(1.0), jnp.tan(theta))
    return jnp.where(skipped, jnp.float32(0.0), 0.5 * parity / safe_tan).astype(jnp.float32)


def wall_plus(field):
    zeros = jnp.zeros_like(field[:, :1])
    return jnp.concatenate([field[:, 1:], zeros], axis=1)


def wall_minus(field):
    zeros = jnp.zeros_like(field[:, :1])
    return jnp.concatenate([zeros, field[:, :-1]], axis=1)


def butterfly_sum(x, axis):
    groups = lax.axis_size(axis)
    bit = 1
    while bit < groups:
        x = x + lax.ppermute(x, axis, [(i, i ^ bit) for i in range(groups)])
        bit *= 2
    return x


def neighbours(slab, axis):
    count = lax.axis_size(axis)
    up = [(i, (i + 1) % count) for i in range(count)]
    down = [(j, i) for i, j in up]
    prev = lax.ppermute(slab, axis, up)
    if count == 2:
        return prev, prev
    return prev, lax.ppermute(slab, axis, down)


def stencil_kernel(pulse_ref, field_ref, vel_ref, src_ref, prev_ref, prev_u_ref, next_ref, next_u_ref, kept_ref, walls_ref):
    nx, cy, cz = field_ref.shape
    row = lax.broadcasted_iota(jnp.int32, (cy, cz), 0)

    def wall_up(a):
        return jnp.where(row == cy - 1, 0.0, pltpu.roll(a, cy - 1, 0))

    def wall_down(a):
        return jnp.where(row == 0, 0.0, pltpu.roll(a, 1, 0))

    def span_up(a):
        return pltpu.roll(a, cz - 1, 1)

    def span_down(a):
        return pltpu.roll(a, 1, 1)

    for x in range(nx):
        f = field_ref[x]
        if x + 1 < nx:
            ahead, ahead_x = field_ref[x + 1], vel_ref[0, x + 1] * field_ref[x + 1]
        else:
            ahead, ahead_x = next_ref[0, 0], next_u_ref[0, 0, 0] * next_ref[0, 0]
        if x > 0:
            behind, behind_x = field_ref[x - 1], vel_ref[0, x - 1] * field_ref[x - 1]
        else:
            behind, behind_x = prev_ref[0, 0], prev_u_ref[0, 0, 0] * prev_ref[0, 0]
        flux_y = vel_ref[1, x] * f
        flux_z = vel_ref[2, x] * f
        advect = 0.5 * (ahead_x - behind_x)
        advect = advect + 0.5 * (wall_up(flux_y) - wall_down(flux_y))
        advect = advect + 0.5 * (span_up(flux_z) - span_down(flux_z))
        beside = ahead + behind
        beside = beside + wall_up(f) + wall_down(f)
        beside = beside + span_up(f) + span_down(f)
        operator = advect + viscosity * (beside - 6.0 * f) - reaction * f
        kept = f + pseudo_step * (operator + src_ref[x])
        kept_ref[x] = kept
        walls_ref[0, x : x + 1, :] = pulse_ref[0] * kept[0:1]
        walls_ref[1, x : x + 1, :] = f[0:1]


def whole(shape):
    return pl.BlockSpec(shape, lambda i: (0,) * len(shape))


def layer(shape, dim, at):
    block = tuple(1 if d == dim else n for d, n in enumerate(shape))
    return pl.BlockSpec(block, lambda i: tuple(at if d == dim else 0 for d in range(len(shape))))


def stencil(pulse, field, velocity, source, prev, nxt):
    nx, cy, cz = field.shape
    slab, flow = prev[0].shape, prev[1].shape
    return pl.pallas_call(
        stencil_kernel,
        grid=(1,),
        out_shape=(
            jax.ShapeDtypeStruct((nx, cy, cz), jnp.float32),
            jax.ShapeDtypeStruct((2, nx, cz), jnp.float32),
        ),
        in_specs=[
            pl.BlockSpec(memory_space=pltpu.SMEM),
            whole(field.shape),
            whole(velocity.shape),
            whole(source.shape),
            layer(slab, 1, nx - 1),
            layer(flow, 2, nx - 1),
            layer(slab, 1, 0),
            layer(flow, 2, 0),
        ],
        out_specs=(whole((nx, cy, cz)), whole((2, nx, cz))),
    )(pulse, field, velocity, source, *prev, *nxt)


def on_device(adjoint, base_flow, source, pulse, actuator):
    count = lax.axis_size("tm")
    nt_loc, nx, cy, cz = adjoint.shape
    total = count * nt_loc
    chunk = nx * cy // count
    share = NACT // count
    pad = 8
    dmat = spectral_matrix(total)

    incoming = lax.all_to_all(adjoint.reshape(count, chunk, cz), "tm", 0, 0, tiled=True)

    field = adjoint[0]
    velocity = base_flow[:, 0]
    prev, nxt = neighbours((adjoint, base_flow), "space")
    kept, walls = stencil(pulse, field, velocity, source[0], prev, nxt)

    onehot = (actuator[:, :, None] == jnp.arange(NACT, dtype=jnp.int32)[None, None, :]).astype(
        jnp.float32
    )
    terms = jnp.dot(
        walls.reshape(2, -1),
        onehot.reshape(-1, NACT),
        precision=lax.Precision.HIGHEST,
        preferred_element_type=jnp.float32,
    )
    terms = butterfly_sum(terms, "space")
    scales = jnp.array([1.0, -pseudo_step * omega_rate], jnp.float32)[:, None] / total
    slices = jnp.transpose((terms * scales).reshape(2, count, share), (1, 0, 2))
    slices = jnp.pad(slices, ((0, 0), (0, 0), (0, cz - share)))
    pulse_row = jnp.broadcast_to(pulse.reshape(1, 1, 1), (count, 1, cz))
    grad_rows = jnp.concatenate([slices, pulse_row, jnp.zeros((count, pad - 3, cz), jnp.float32)], axis=1)
    kept, grad_rows, incoming = lax.optimization_barrier((kept, grad_rows, incoming))
    derived = jnp.einsum(
        "ji,jrc->irc",
        (-pseudo_step * omega_rate) * dmat,
        incoming,
        precision=lax.Precision.HIGHEST,
    )

    outgoing = jnp.concatenate([derived, grad_rows], axis=1)
    incoming = lax.all_to_all(outgoing, "tm", 0, 0, tiled=True)
    scaled_term = incoming[:, :chunk].reshape(nx, cy, cz)
    tile = incoming[:, chunk : chunk + 3, :share]
    weights = jnp.sum(dmat * tile[None, :, 2, 0], axis=1)
    gradient = jnp.sum(tile[:, 0] + weights[:, None] * tile[:, 1], axis=0)
    updated = kept + scaled_term
    return (updated[None], gradient)


def solution(mesh):
    in_specs = (
        P("tm", "space", None, None),
        P(None, "tm", "space", None, None),
        P("tm", "space", None, None),
        P("tm"),
        P("space", None),
    )
    out_specs = (P("tm", "space", None, None), P("tm"))
    return jax.shard_map(
        on_device, mesh=mesh, in_specs=in_specs, out_specs=out_specs, check_vma=False
    )
```

```python
import math

import jax
import jax.numpy as jnp
from jax import lax
from jax.experimental import pallas as pl
from jax.experimental.pallas import tpu as pltpu
from jax.sharding import PartitionSpec as P

NACT = 128


omega_rate = 0.25
pseudo_step = 0.2
viscosity = 0.2
reaction = 0.5


def spectral_matrix(count):
    steps = jnp.arange(count, dtype=jnp.int32)
    offset = steps[:, None] - steps[None, :]
    theta = math.pi * offset.astype(jnp.float32) / count
    parity = jnp.where(offset % 2 == 0, 1.0, -1.0).astype(jnp.float32)
    skipped = (offset == 0) | (jnp.abs(offset) == count // 2)
    safe_tan = jnp.where(skipped, jnp.float32(1.0), jnp.tan(theta))
    return jnp.where(skipped, jnp.float32(0.0), 0.5 * parity / safe_tan).astype(jnp.float32)


def wall_plus(field):
    zeros = jnp.zeros_like(field[:, :1])
    return jnp.concatenate([field[:, 1:], zeros], axis=1)


def wall_minus(field):
    zeros = jnp.zeros_like(field[:, :1])
    return jnp.concatenate([zeros, field[:, :-1]], axis=1)


def butterfly_sum(x, axis):
    groups = lax.axis_size(axis)
    bit = 1
    while bit < groups:
        x = x + lax.ppermute(x, axis, [(i, i ^ bit) for i in range(groups)])
        bit *= 2
    return x


def neighbours(slab, axis):
    count = lax.axis_size(axis)
    up = [(i, (i + 1) % count) for i in range(count)]
    down = [(j, i) for i, j in up]
    prev = lax.ppermute(slab, axis, up)
    if count == 2:
        return prev, prev
    return prev, lax.ppermute(slab, axis, down)


def stencil_kernel(pulse_ref, field_ref, vel_ref, src_ref, prev_ref, prev_u_ref, next_ref, next_u_ref, kept_ref, walls_ref):
    nx, cy, cz = field_ref.shape
    row = lax.broadcasted_iota(jnp.int32, (cy, cz), 0)

    def wall_up(a):
        return jnp.where(row == cy - 1, 0.0, pltpu.roll(a, cy - 1, 0))

    def wall_down(a):
        return jnp.where(row == 0, 0.0, pltpu.roll(a, 1, 0))

    def span_up(a):
        return pltpu.roll(a, cz - 1, 1)

    def span_down(a):
        return pltpu.roll(a, 1, 1)

    for x in range(nx):
        f = field_ref[x]
        if x + 1 < nx:
            ahead, ahead_x = field_ref[x + 1], vel_ref[0, x + 1] * field_ref[x + 1]
        else:
            ahead, ahead_x = next_ref[0, 0], next_u_ref[0, 0, 0] * next_ref[0, 0]
        if x > 0:
            behind, behind_x = field_ref[x - 1], vel_ref[0, x - 1] * field_ref[x - 1]
        else:
            behind, behind_x = prev_ref[0, 0], prev_u_ref[0, 0, 0] * prev_ref[0, 0]
        flux_y = vel_ref[1, x] * f
        flux_z = vel_ref[2, x] * f
        advect = 0.5 * (ahead_x - behind_x)
        advect = advect + 0.5 * (wall_up(flux_y) - wall_down(flux_y))
        advect = advect + 0.5 * (span_up(flux_z) - span_down(flux_z))
        beside = ahead + behind
        beside = beside + wall_up(f) + wall_down(f)
        beside = beside + span_up(f) + span_down(f)
        operator = advect + viscosity * (beside - 6.0 * f) - reaction * f
        kept = f + pseudo_step * (operator + src_ref[x])
        kept_ref[x] = kept
        walls_ref[0, x : x + 1, :] = pulse_ref[0] * kept[0:1]
        walls_ref[1, x : x + 1, :] = f[0:1]


def whole(shape):
    return pl.BlockSpec(shape, lambda i: (0,) * len(shape))


def layer(shape, dim, at):
    block = tuple(1 if d == dim else n for d, n in enumerate(shape))
    return pl.BlockSpec(block, lambda i: tuple(at if d == dim else 0 for d in range(len(shape))))


def stencil(pulse, field, velocity, source, prev, nxt):
    nx, cy, cz = field.shape
    slab, flow = prev[0].shape, prev[1].shape
    return pl.pallas_call(
        stencil_kernel,
        grid=(1,),
        out_shape=(
            jax.ShapeDtypeStruct((nx, cy, cz), jnp.float32),
            jax.ShapeDtypeStruct((2, nx, cz), jnp.float32),
        ),
        in_specs=[
            pl.BlockSpec(memory_space=pltpu.SMEM),
            whole(field.shape),
            whole(velocity.shape),
            whole(source.shape),
            layer(slab, 1, nx - 1),
            layer(flow, 2, nx - 1),
            layer(slab, 1, 0),
            layer(flow, 2, 0),
        ],
        out_specs=(whole((nx, cy, cz)), whole((2, nx, cz))),
    )(pulse, field, velocity, source, *prev, *nxt)


def finish_kernel(dmat_ref, term_ref, tile_ref, kept_ref, out_ref, grad_ref):
    block, chunk, cz = term_ref.shape
    out_ref[...] = kept_ref[...] + term_ref[...].reshape(block * chunk, cz)

    @pl.when(pl.program_id(0) == 0)
    def _():
        count = tile_ref.shape[0]
        pulses = tile_ref[:, 2, :]
        weights = jnp.zeros((count, cz), jnp.float32)
        for i in range(count):
            weights = weights + dmat_ref[:, i : i + 1] * pulses[i : i + 1, :]
        parts = tile_ref[:, 0, :] + weights * tile_ref[:, 1, :]
        grad_ref[...] = jnp.sum(parts, axis=0, keepdims=True)[0, : grad_ref.shape[0]]


def finish(dmat, incoming, kept, share):
    count, width, cz = incoming.shape
    chunk = width - 8
    rows = kept.shape[0]
    steps = 4 if count % 4 == 0 else 1
    return pl.pallas_call(
        finish_kernel,
        grid=(steps,),
        out_shape=(
            jax.ShapeDtypeStruct((rows, cz), jnp.float32),
            jax.ShapeDtypeStruct((share,), jnp.float32),
        ),
        in_specs=[
            pl.BlockSpec((count, count), lambda s: (0, 0)),
            pl.BlockSpec((count // steps, chunk, cz), lambda s: (s, 0, 0)),
            pl.BlockSpec((count, 8, cz), lambda s: (0, chunk // 8, 0)),
            pl.BlockSpec((rows // steps, cz), lambda s: (s, 0)),
        ],
        out_specs=(
            pl.BlockSpec((rows // steps, cz), lambda s: (s, 0)),
            pl.BlockSpec((share,), lambda s: (0,)),
        ),
    )(dmat, incoming, incoming, kept)


def on_device(adjoint, base_flow, source, pulse, actuator):
    count = lax.axis_size("tm")
    nt_loc, nx, cy, cz = adjoint.shape
    total = count * nt_loc
    chunk = nx * cy // count
    share = NACT // count
    pad = 8
    dmat = spectral_matrix(total)

    incoming = lax.all_to_all(adjoint.reshape(count, chunk, cz), "tm", 0, 0, tiled=True)

    field = adjoint[0]
    velocity = base_flow[:, 0]
    prev, nxt = neighbours((adjoint, base_flow), "space")
    kept, walls = stencil(pulse, field, velocity, source[0], prev, nxt)

    onehot = (actuator[:, :, None] == jnp.arange(NACT, dtype=jnp.int32)[None, None, :]).astype(
        jnp.float32
    )
    terms = jnp.dot(
        walls.reshape(2, -1),
        onehot.reshape(-1, NACT),
        precision=lax.Precision.HIGHEST,
        preferred_element_type=jnp.float32,
    )
    terms = butterfly_sum(terms, "space")
    scales = jnp.array([1.0, -pseudo_step * omega_rate], jnp.float32)[:, None] / total
    slices = jnp.transpose((terms * scales).reshape(2, count, share), (1, 0, 2))
    slices = jnp.pad(slices, ((0, 0), (0, 0), (0, cz - share)))
    pulse_row = jnp.broadcast_to(pulse.reshape(1, 1, 1), (count, 1, cz))
    grad_rows = jnp.concatenate([slices, pulse_row, jnp.zeros((count, pad - 3, cz), jnp.float32)], axis=1)
    kept, grad_rows, incoming = lax.optimization_barrier((kept, grad_rows, incoming))
    derived = jnp.einsum(
        "ji,jrc->irc",
        (-pseudo_step * omega_rate) * dmat,
        incoming,
        precision=lax.Precision.HIGHEST,
    )

    outgoing = jnp.concatenate([derived, grad_rows], axis=1)
    incoming = lax.all_to_all(outgoing, "tm", 0, 0, tiled=True)
    updated, gradient = finish(dmat, incoming, kept.reshape(nx * cy, cz), share)
    updated = updated.reshape(nx, cy, cz)
    return (updated[None], gradient)


def solution(mesh):
    in_specs = (
        P("tm", "space", None, None),
        P(None, "tm", "space", None, None),
        P("tm", "space", None, None),
        P("tm"),
        P("space", None),
    )
    out_specs = (P("tm", "space", None, None), P("tm"))
    return jax.shard_map(
        on_device, mesh=mesh, in_specs=in_specs, out_specs=out_specs, check_vma=False
    )
```

```python
import math

import jax
import jax.numpy as jnp
from jax import lax
from jax.experimental import pallas as pl
from jax.experimental.pallas import tpu as pltpu
from jax.sharding import PartitionSpec as P

NACT = 128


omega_rate = 0.25
pseudo_step = 0.2
viscosity = 0.2
reaction = 0.5


def spectral_matrix(count):
    steps = jnp.arange(count, dtype=jnp.int32)
    offset = steps[:, None] - steps[None, :]
    theta = math.pi * offset.astype(jnp.float32) / count
    parity = jnp.where(offset % 2 == 0, 1.0, -1.0).astype(jnp.float32)
    skipped = (offset == 0) | (jnp.abs(offset) == count // 2)
    safe_tan = jnp.where(skipped, jnp.float32(1.0), jnp.tan(theta))
    return jnp.where(skipped, jnp.float32(0.0), 0.5 * parity / safe_tan).astype(jnp.float32)


def wall_plus(field):
    zeros = jnp.zeros_like(field[:, :1])
    return jnp.concatenate([field[:, 1:], zeros], axis=1)


def wall_minus(field):
    zeros = jnp.zeros_like(field[:, :1])
    return jnp.concatenate([zeros, field[:, :-1]], axis=1)


def butterfly_sum(x, axis):
    groups = lax.axis_size(axis)
    bit = 1
    while bit < groups:
        x = x + lax.ppermute(x, axis, [(i, i ^ bit) for i in range(groups)])
        bit *= 2
    return x


def neighbours(slab, axis):
    count = lax.axis_size(axis)
    up = [(i, (i + 1) % count) for i in range(count)]
    down = [(j, i) for i, j in up]
    prev = lax.ppermute(slab, axis, up)
    if count == 2:
        return prev, prev
    return prev, lax.ppermute(slab, axis, down)


def stencil_kernel(pulse_ref, field_ref, vel_ref, src_ref, prev_ref, prev_u_ref, next_ref, next_u_ref, kept_ref, walls_ref):
    nx, cy, cz = field_ref.shape
    row = lax.broadcasted_iota(jnp.int32, (cy, cz), 0)

    def wall_up(a):
        return jnp.where(row == cy - 1, 0.0, pltpu.roll(a, cy - 1, 0))

    def wall_down(a):
        return jnp.where(row == 0, 0.0, pltpu.roll(a, 1, 0))

    def span_up(a):
        return pltpu.roll(a, cz - 1, 1)

    def span_down(a):
        return pltpu.roll(a, 1, 1)

    for x in range(nx):
        f = field_ref[x]
        if x + 1 < nx:
            ahead, ahead_x = field_ref[x + 1], vel_ref[0, x + 1] * field_ref[x + 1]
        else:
            ahead, ahead_x = next_ref[0, 0], next_u_ref[0, 0, 0] * next_ref[0, 0]
        if x > 0:
            behind, behind_x = field_ref[x - 1], vel_ref[0, x - 1] * field_ref[x - 1]
        else:
            behind, behind_x = prev_ref[0, 0], prev_u_ref[0, 0, 0] * prev_ref[0, 0]
        flux_y = vel_ref[1, x] * f
        flux_z = vel_ref[2, x] * f
        advect = 0.5 * (ahead_x - behind_x)
        advect = advect + 0.5 * (wall_up(flux_y) - wall_down(flux_y))
        advect = advect + 0.5 * (span_up(flux_z) - span_down(flux_z))
        beside = ahead + behind
        beside = beside + wall_up(f) + wall_down(f)
        beside = beside + span_up(f) + span_down(f)
        operator = advect + viscosity * (beside - 6.0 * f) - reaction * f
        kept = f + pseudo_step * (operator + src_ref[x])
        kept_ref[x] = kept
        walls_ref[0, x : x + 1, :] = pulse_ref[0] * kept[0:1]
        walls_ref[1, x : x + 1, :] = f[0:1]


def whole(shape):
    return pl.BlockSpec(shape, lambda i: (0,) * len(shape))


def layer(shape, dim, at):
    block = tuple(1 if d == dim else n for d, n in enumerate(shape))
    return pl.BlockSpec(block, lambda i: tuple(at if d == dim else 0 for d in range(len(shape))))


def stencil(pulse, field, velocity, source, prev, nxt):
    nx, cy, cz = field.shape
    slab, flow = prev[0].shape, prev[1].shape
    return pl.pallas_call(
        stencil_kernel,
        grid=(1,),
        out_shape=(
            jax.ShapeDtypeStruct((nx, cy, cz), jnp.float32),
            jax.ShapeDtypeStruct((2, nx, cz), jnp.float32),
        ),
        in_specs=[
            pl.BlockSpec(memory_space=pltpu.SMEM),
            whole(field.shape),
            whole(velocity.shape),
            whole(source.shape),
            layer(slab, 1, nx - 1),
            layer(flow, 2, nx - 1),
            layer(slab, 1, 0),
            layer(flow, 2, 0),
        ],
        out_specs=(whole((nx, cy, cz)), whole((2, nx, cz))),
    )(pulse, field, velocity, source, *prev, *nxt)


def on_device(adjoint, base_flow, source, pulse, actuator):
    count = lax.axis_size("tm")
    nt_loc, nx, cy, cz = adjoint.shape
    total = count * nt_loc
    chunk = nx * cy // count
    share = NACT // count
    pad = 8
    dmat = spectral_matrix(total)

    incoming = lax.all_to_all(adjoint.reshape(count, chunk, cz), "tm", 0, 0, tiled=True)

    field = adjoint[0]
    velocity = base_flow[:, 0]
    prev, nxt = neighbours((adjoint, base_flow), "space")
    kept, walls = stencil(pulse, field, velocity, source[0], prev, nxt)

    onehot = (actuator[:, :, None] == jnp.arange(NACT, dtype=jnp.int32)[None, None, :]).astype(
        jnp.float32
    )
    terms = jnp.dot(
        walls.reshape(2, -1),
        onehot.reshape(-1, NACT),
        precision=lax.Precision.HIGHEST,
        preferred_element_type=jnp.float32,
    )
    terms = butterfly_sum(terms, "space")
    scales = jnp.array([1.0, -pseudo_step * omega_rate], jnp.float32)[:, None] / total
    slices = jnp.transpose((terms * scales).reshape(2, count, share), (1, 0, 2))
    slices = jnp.pad(slices, ((0, 0), (0, 0), (0, cz - share)))
    pulse_row = jnp.broadcast_to(pulse.reshape(1, 1, 1), (count, 1, cz))
    grad_rows = jnp.concatenate([slices, pulse_row, jnp.zeros((count, pad - 3, cz), jnp.float32)], axis=1)
    kept, grad_rows, incoming = lax.optimization_barrier((kept, grad_rows, incoming))
    derived = jnp.einsum(
        "ji,jrc->irc",
        (-pseudo_step * omega_rate) * dmat,
        incoming,
        precision=lax.Precision.HIGHEST,
    )

    outgoing = jnp.concatenate([derived, grad_rows], axis=1)
    incoming = lax.all_to_all(outgoing, "tm", 0, 0, tiled=True)
    scaled_term = incoming[:, :chunk].reshape(nx, cy, cz)
    weights = jnp.sum(dmat * incoming[None, :, chunk + 2, 0], axis=1)
    lanes = incoming[:, chunk, :] + weights[:, None] * incoming[:, chunk + 1, :]
    gradient = jnp.sum(lanes, axis=0)[:share]
    updated = kept + scaled_term
    return (updated[None], gradient)


def solution(mesh):
    in_specs = (
        P("tm", "space", None, None),
        P(None, "tm", "space", None, None),
        P("tm", "space", None, None),
        P("tm"),
        P("space", None),
    )
    out_specs = (P("tm", "space", None, None), P("tm"))
    return jax.shard_map(
        on_device, mesh=mesh, in_specs=in_specs, out_specs=out_specs, check_vma=False
    )
```

```python
import math

import jax
import jax.numpy as jnp
from jax import lax
from jax.experimental import pallas as pl
from jax.experimental.pallas import tpu as pltpu
from jax.sharding import PartitionSpec as P

NACT = 128


omega_rate = 0.25
pseudo_step = 0.2
viscosity = 0.2
reaction = 0.5


def spectral_matrix(count):
    steps = jnp.arange(count, dtype=jnp.int32)
    offset = steps[:, None] - steps[None, :]
    theta = math.pi * offset.astype(jnp.float32) / count
    parity = jnp.where(offset % 2 == 0, 1.0, -1.0).astype(jnp.float32)
    skipped = (offset == 0) | (jnp.abs(offset) == count // 2)
    safe_tan = jnp.where(skipped, jnp.float32(1.0), jnp.tan(theta))
    return jnp.where(skipped, jnp.float32(0.0), 0.5 * parity / safe_tan).astype(jnp.float32)


def wall_plus(field):
    zeros = jnp.zeros_like(field[:, :1])
    return jnp.concatenate([field[:, 1:], zeros], axis=1)


def wall_minus(field):
    zeros = jnp.zeros_like(field[:, :1])
    return jnp.concatenate([zeros, field[:, :-1]], axis=1)


def butterfly_sum(x, axis):
    groups = lax.axis_size(axis)
    bit = 1
    while bit < groups:
        x = x + lax.ppermute(x, axis, [(i, i ^ bit) for i in range(groups)])
        bit *= 2
    return x


def neighbours(slab, axis):
    count = lax.axis_size(axis)
    up = [(i, (i + 1) % count) for i in range(count)]
    down = [(j, i) for i, j in up]
    prev = lax.ppermute(slab, axis, up)
    if count == 2:
        return prev, prev
    return prev, lax.ppermute(slab, axis, down)


def stencil_kernel(pulse_ref, field_ref, vel_ref, src_ref, prev_ref, prev_u_ref, next_ref, next_u_ref, kept_ref, walls_ref):
    nx, cy, cz = field_ref.shape
    row = lax.broadcasted_iota(jnp.int32, (cy, cz), 0)

    def wall_up(a):
        return jnp.where(row == cy - 1, 0.0, pltpu.roll(a, cy - 1, 0))

    def wall_down(a):
        return jnp.where(row == 0, 0.0, pltpu.roll(a, 1, 0))

    def span_up(a):
        return pltpu.roll(a, cz - 1, 1)

    def span_down(a):
        return pltpu.roll(a, 1, 1)

    for x in range(nx):
        f = field_ref[x]
        if x + 1 < nx:
            ahead, ahead_x = field_ref[x + 1], vel_ref[0, x + 1] * field_ref[x + 1]
        else:
            ahead, ahead_x = next_ref[0, 0], next_u_ref[0, 0, 0] * next_ref[0, 0]
        if x > 0:
            behind, behind_x = field_ref[x - 1], vel_ref[0, x - 1] * field_ref[x - 1]
        else:
            behind, behind_x = prev_ref[0, 0], prev_u_ref[0, 0, 0] * prev_ref[0, 0]
        flux_y = vel_ref[1, x] * f
        flux_z = vel_ref[2, x] * f
        advect = 0.5 * (ahead_x - behind_x)
        advect = advect + 0.5 * (wall_up(flux_y) - wall_down(flux_y))
        advect = advect + 0.5 * (span_up(flux_z) - span_down(flux_z))
        beside = ahead + behind
        beside = beside + wall_up(f) + wall_down(f)
        beside = beside + span_up(f) + span_down(f)
        operator = advect + viscosity * (beside - 6.0 * f) - reaction * f
        kept = f + pseudo_step * (operator + src_ref[x])
        kept_ref[x] = kept
        walls_ref[0, x : x + 1, :] = pulse_ref[0] * kept[0:1]
        walls_ref[1, x : x + 1, :] = f[0:1]


def whole(shape):
    return pl.BlockSpec(shape, lambda i: (0,) * len(shape))


def layer(shape, dim, at):
    block = tuple(1 if d == dim else n for d, n in enumerate(shape))
    return pl.BlockSpec(block, lambda i: tuple(at if d == dim else 0 for d in range(len(shape))))


def stencil(pulse, field, velocity, source, prev, nxt):
    nx, cy, cz = field.shape
    slab, flow = prev[0].shape, prev[1].shape
    return pl.pallas_call(
        stencil_kernel,
        grid=(1,),
        out_shape=(
            jax.ShapeDtypeStruct((nx, cy, cz), jnp.float32),
            jax.ShapeDtypeStruct((2, nx, cz), jnp.float32),
        ),
        in_specs=[
            pl.BlockSpec(memory_space=pltpu.SMEM),
            whole(field.shape),
            whole(velocity.shape),
            whole(source.shape),
            layer(slab, 1, nx - 1),
            layer(flow, 2, nx - 1),
            layer(slab, 1, 0),
            layer(flow, 2, 0),
        ],
        out_specs=(whole((nx, cy, cz)), whole((2, nx, cz))),
    )(pulse, field, velocity, source, *prev, *nxt)


def on_device(adjoint, base_flow, source, pulse, actuator):
    count = lax.axis_size("tm")
    nt_loc, nx, cy, cz = adjoint.shape
    total = count * nt_loc
    chunk = nx * cy // count
    share = NACT // count
    pad = 8
    dmat = spectral_matrix(total)

    incoming = lax.all_to_all(adjoint.reshape(count, chunk, cz), "tm", 0, 0, tiled=True)

    field = adjoint[0]
    velocity = base_flow[:, 0]
    prev, nxt = neighbours((adjoint, base_flow), "space")
    kept, walls = stencil(pulse, field, velocity, source[0], prev, nxt)

    onehot = (actuator[:, :, None] == jnp.arange(NACT, dtype=jnp.int32)[None, None, :]).astype(
        jnp.float32
    )
    terms = jnp.dot(
        walls.reshape(2, -1),
        onehot.reshape(-1, NACT),
        precision=lax.Precision.HIGHEST,
        preferred_element_type=jnp.float32,
    )
    terms = butterfly_sum(terms, "space")
    position = lax.axis_index("tm")
    scales = jnp.array([1.0, -pseudo_step * omega_rate], jnp.float32)[:, None] / total
    scaled = (terms * scales).reshape(2, count, share)
    own_row = lax.dynamic_index_in_dim(dmat, position, 0, keepdims=False)
    spread = (own_row[None, :, None] * scaled[1][:, None, :]).reshape(count, NACT)
    mine = jnp.where(jnp.arange(count) == position, pulse[0], 0.0)
    pulse_lanes = jnp.broadcast_to(jnp.repeat(mine, share)[None, :], (count, NACT))
    rows = jnp.stack([jnp.pad(scaled[0], ((0, 0), (0, NACT - share))), spread, pulse_lanes], axis=1)
    rows = jnp.pad(rows, ((0, 0), (0, 0), (0, cz - NACT)))
    grad_rows = jnp.concatenate([rows, jnp.zeros((count, pad - 3, cz), jnp.float32)], axis=1)
    kept, grad_rows, incoming = lax.optimization_barrier((kept, grad_rows, incoming))
    derived = jnp.einsum(
        "ji,jrc->irc",
        (-pseudo_step * omega_rate) * dmat,
        incoming,
        precision=lax.Precision.HIGHEST,
    )

    outgoing = jnp.concatenate([derived, grad_rows], axis=1)
    incoming = lax.all_to_all(outgoing, "tm", 0, 0, tiled=True)
    scaled_term = incoming[:, :chunk].reshape(nx, cy, cz)
    sums = jnp.sum(incoming[:, chunk : chunk + 3, :NACT], axis=0)
    gradient = sums[0, :share] + jnp.sum((sums[1] * sums[2]).reshape(count, share), axis=0)
    updated = kept + scaled_term
    return (updated[None], gradient)


def solution(mesh):
    in_specs = (
        P("tm", "space", None, None),
        P(None, "tm", "space", None, None),
        P("tm", "space", None, None),
        P("tm"),
        P("space", None),
    )
    out_specs = (P("tm", "space", None, None), P("tm"))
    return jax.shard_map(
        on_device, mesh=mesh, in_specs=in_specs, out_specs=out_specs, check_vma=False
    )
```

```python
import math

import jax
import jax.numpy as jnp
from jax import lax
from jax.experimental import pallas as pl
from jax.experimental.pallas import tpu as pltpu
from jax.sharding import PartitionSpec as P

NACT = 128


omega_rate = 0.25
pseudo_step = 0.2
viscosity = 0.2
reaction = 0.5


def spectral_matrix(count):
    steps = jnp.arange(count, dtype=jnp.int32)
    offset = steps[:, None] - steps[None, :]
    theta = math.pi * offset.astype(jnp.float32) / count
    parity = jnp.where(offset % 2 == 0, 1.0, -1.0).astype(jnp.float32)
    skipped = (offset == 0) | (jnp.abs(offset) == count // 2)
    safe_tan = jnp.where(skipped, jnp.float32(1.0), jnp.tan(theta))
    return jnp.where(skipped, jnp.float32(0.0), 0.5 * parity / safe_tan).astype(jnp.float32)


def wall_plus(field):
    zeros = jnp.zeros_like(field[:, :1])
    return jnp.concatenate([field[:, 1:], zeros], axis=1)


def wall_minus(field):
    zeros = jnp.zeros_like(field[:, :1])
    return jnp.concatenate([zeros, field[:, :-1]], axis=1)


def butterfly_sum(x, axis):
    groups = lax.axis_size(axis)
    bit = 1
    while bit < groups:
        x = x + lax.ppermute(x, axis, [(i, i ^ bit) for i in range(groups)])
        bit *= 2
    return x


def neighbours(slab, axis):
    count = lax.axis_size(axis)
    up = [(i, (i + 1) % count) for i in range(count)]
    down = [(j, i) for i, j in up]
    prev = lax.ppermute(slab, axis, up)
    if count == 2:
        return prev, prev
    return prev, lax.ppermute(slab, axis, down)


def stencil_kernel(pulse_ref, field_ref, vel_ref, src_ref, prev_ref, prev_u_ref, next_ref, next_u_ref, kept_ref, walls_ref):
    nx, cy, cz = field_ref.shape
    row = lax.broadcasted_iota(jnp.int32, (cy, cz), 0)

    def wall_up(a):
        return jnp.where(row == cy - 1, 0.0, pltpu.roll(a, cy - 1, 0))

    def wall_down(a):
        return jnp.where(row == 0, 0.0, pltpu.roll(a, 1, 0))

    def span_up(a):
        return pltpu.roll(a, cz - 1, 1)

    def span_down(a):
        return pltpu.roll(a, 1, 1)

    for x in range(nx):
        f = field_ref[x]
        if x + 1 < nx:
            ahead, ahead_x = field_ref[x + 1], vel_ref[0, x + 1] * field_ref[x + 1]
        else:
            ahead, ahead_x = next_ref[0, 0], next_u_ref[0, 0, 0] * next_ref[0, 0]
        if x > 0:
            behind, behind_x = field_ref[x - 1], vel_ref[0, x - 1] * field_ref[x - 1]
        else:
            behind, behind_x = prev_ref[0, 0], prev_u_ref[0, 0, 0] * prev_ref[0, 0]
        flux_y = vel_ref[1, x] * f
        flux_z = vel_ref[2, x] * f
        advect = 0.5 * (ahead_x - behind_x)
        advect = advect + 0.5 * (wall_up(flux_y) - wall_down(flux_y))
        advect = advect + 0.5 * (span_up(flux_z) - span_down(flux_z))
        beside = ahead + behind
        beside = beside + wall_up(f) + wall_down(f)
        beside = beside + span_up(f) + span_down(f)
        operator = advect + viscosity * (beside - 6.0 * f) - reaction * f
        kept = f + pseudo_step * (operator + src_ref[x])
        kept_ref[x] = kept
        walls_ref[0, x : x + 1, :] = pulse_ref[0] * kept[0:1]
        walls_ref[1, x : x + 1, :] = f[0:1]


def whole(shape):
    return pl.BlockSpec(shape, lambda i: (0,) * len(shape))


def layer(shape, dim, at):
    block = tuple(1 if d == dim else n for d, n in enumerate(shape))
    return pl.BlockSpec(block, lambda i: tuple(at if d == dim else 0 for d in range(len(shape))))


def stencil(pulse, field, velocity, source, prev, nxt):
    nx, cy, cz = field.shape
    slab, flow = prev[0].shape, prev[1].shape
    return pl.pallas_call(
        stencil_kernel,
        grid=(1,),
        out_shape=(
            jax.ShapeDtypeStruct((nx, cy, cz), jnp.float32),
            jax.ShapeDtypeStruct((2, nx, cz), jnp.float32),
        ),
        in_specs=[
            pl.BlockSpec(memory_space=pltpu.SMEM),
            whole(field.shape),
            whole(velocity.shape),
            whole(source.shape),
            layer(slab, 1, nx - 1),
            layer(flow, 2, nx - 1),
            layer(slab, 1, 0),
            layer(flow, 2, 0),
        ],
        out_specs=(whole((nx, cy, cz)), whole((2, nx, cz))),
    )(pulse, field, velocity, source, *prev, *nxt)


def on_device(adjoint, base_flow, source, pulse, actuator):
    count = lax.axis_size("tm")
    nt_loc, nx, cy, cz = adjoint.shape
    total = count * nt_loc
    chunk = nx * cy // count
    share = NACT // count
    pad = 8
    dmat = spectral_matrix(total)

    incoming = lax.all_to_all(adjoint.reshape(count, chunk, cz), "tm", 0, 0, tiled=True)

    field = adjoint[0]
    velocity = base_flow[:, 0]
    prev, nxt = neighbours((adjoint, base_flow), "space")
    kept, walls = stencil(pulse, field, velocity, source[0], prev, nxt)

    onehot = (actuator[:, :, None] == jnp.arange(NACT, dtype=jnp.int32)[None, None, :]).astype(
        jnp.float32
    )
    terms = jnp.dot(
        walls.reshape(2, -1),
        onehot.reshape(-1, NACT),
        precision=lax.Precision.HIGHEST,
        preferred_element_type=jnp.float32,
    )
    terms = butterfly_sum(terms, "space")
    scales = jnp.array([1.0, -pseudo_step * omega_rate], jnp.float32)[:, None] / total
    slices = jnp.transpose((terms * scales).reshape(2, count, share), (1, 0, 2))
    slices = jnp.pad(slices, ((0, 0), (0, 0), (0, cz - share)))
    pulse_row = jnp.broadcast_to(pulse.reshape(1, 1, 1), (count, 1, cz))
    grad_rows = jnp.concatenate([slices, pulse_row, jnp.zeros((count, pad - 3, cz), jnp.float32)], axis=1)
    kept, grad_rows, incoming = lax.optimization_barrier((kept, grad_rows, incoming))
    weighted = (-pseudo_step * omega_rate) * dmat
    derived = jnp.sum(weighted[:, :, None, None] * incoming[:, None], axis=0)

    outgoing = jnp.concatenate([derived, grad_rows], axis=1)
    incoming = lax.all_to_all(outgoing, "tm", 0, 0, tiled=True)
    scaled_term = incoming[:, :chunk].reshape(nx, cy, cz)
    weights = jnp.sum(dmat * incoming[None, :, chunk + 2, 0], axis=1)
    lanes = incoming[:, chunk, :] + weights[:, None] * incoming[:, chunk + 1, :]
    gradient = jnp.sum(lanes, axis=0)[:share]
    updated = kept + scaled_term
    return (updated[None], gradient)


def solution(mesh):
    in_specs = (
        P("tm", "space", None, None),
        P(None, "tm", "space", None, None),
        P("tm", "space", None, None),
        P("tm"),
        P("space", None),
    )
    out_specs = (P("tm", "space", None, None), P("tm"))
    return jax.shard_map(
        on_device, mesh=mesh, in_specs=in_specs, out_specs=out_specs, check_vma=False
    )
```

```python
import math

import jax
import jax.numpy as jnp
from jax import lax
from jax.experimental import pallas as pl
from jax.experimental.pallas import tpu as pltpu
from jax.sharding import PartitionSpec as P

NACT = 128


omega_rate = 0.25
pseudo_step = 0.2
viscosity = 0.2
reaction = 0.5


def spectral_matrix(count):
    steps = jnp.arange(count, dtype=jnp.int32)
    offset = steps[:, None] - steps[None, :]
    theta = math.pi * offset.astype(jnp.float32) / count
    parity = jnp.where(offset % 2 == 0, 1.0, -1.0).astype(jnp.float32)
    skipped = (offset == 0) | (jnp.abs(offset) == count // 2)
    safe_tan = jnp.where(skipped, jnp.float32(1.0), jnp.tan(theta))
    return jnp.where(skipped, jnp.float32(0.0), 0.5 * parity / safe_tan).astype(jnp.float32)


def wall_plus(field):
    zeros = jnp.zeros_like(field[:, :1])
    return jnp.concatenate([field[:, 1:], zeros], axis=1)


def wall_minus(field):
    zeros = jnp.zeros_like(field[:, :1])
    return jnp.concatenate([zeros, field[:, :-1]], axis=1)


def butterfly_sum(x, axis):
    groups = lax.axis_size(axis)
    bit = 1
    while bit < groups:
        x = x + lax.ppermute(x, axis, [(i, i ^ bit) for i in range(groups)])
        bit *= 2
    return x


def neighbours(slab, axis):
    count = lax.axis_size(axis)
    up = [(i, (i + 1) % count) for i in range(count)]
    down = [(j, i) for i, j in up]
    prev = lax.ppermute(slab, axis, up)
    if count == 2:
        return prev, prev
    return prev, lax.ppermute(slab, axis, down)


def stencil_kernel(pulse_ref, field_ref, vel_ref, src_ref, prev_ref, prev_u_ref, next_ref, next_u_ref, kept_ref, walls_ref):
    nx, cy, cz = field_ref.shape
    row = lax.broadcasted_iota(jnp.int32, (cy, cz), 0)

    def wall_up(a):
        return jnp.where(row == cy - 1, 0.0, pltpu.roll(a, cy - 1, 0))

    def wall_down(a):
        return jnp.where(row == 0, 0.0, pltpu.roll(a, 1, 0))

    def span_up(a):
        return pltpu.roll(a, cz - 1, 1)

    def span_down(a):
        return pltpu.roll(a, 1, 1)

    for x in range(nx):
        f = field_ref[x]
        if x + 1 < nx:
            ahead, ahead_x = field_ref[x + 1], vel_ref[0, x + 1] * field_ref[x + 1]
        else:
            ahead, ahead_x = next_ref[0, 0], next_u_ref[0, 0, 0] * next_ref[0, 0]
        if x > 0:
            behind, behind_x = field_ref[x - 1], vel_ref[0, x - 1] * field_ref[x - 1]
        else:
            behind, behind_x = prev_ref[0, 0], prev_u_ref[0, 0, 0] * prev_ref[0, 0]
        flux_y = vel_ref[1, x] * f
        flux_z = vel_ref[2, x] * f
        advect = 0.5 * (ahead_x - behind_x)
        advect = advect + 0.5 * (wall_up(flux_y) - wall_down(flux_y))
        advect = advect + 0.5 * (span_up(flux_z) - span_down(flux_z))
        beside = ahead + behind
        beside = beside + wall_up(f) + wall_down(f)
        beside = beside + span_up(f) + span_down(f)
        operator = advect + viscosity * (beside - 6.0 * f) - reaction * f
        kept = f + pseudo_step * (operator + src_ref[x])
        kept_ref[x] = kept
        walls_ref[0, x : x + 1, :] = pulse_ref[0] * kept[0:1]
        walls_ref[1, x : x + 1, :] = f[0:1]


def whole(shape):
    return pl.BlockSpec(shape, lambda i: (0,) * len(shape))


def layer(shape, dim, at):
    block = tuple(1 if d == dim else n for d, n in enumerate(shape))
    return pl.BlockSpec(block, lambda i: tuple(at if d == dim else 0 for d in range(len(shape))))


def stencil(pulse, field, velocity, source, prev, nxt):
    nx, cy, cz = field.shape
    slab, flow = prev[0].shape, prev[1].shape
    return pl.pallas_call(
        stencil_kernel,
        grid=(1,),
        out_shape=(
            jax.ShapeDtypeStruct((nx, cy, cz), jnp.float32),
            jax.ShapeDtypeStruct((2, nx, cz), jnp.float32),
        ),
        in_specs=[
            pl.BlockSpec(memory_space=pltpu.SMEM),
            whole(field.shape),
            whole(velocity.shape),
            whole(source.shape),
            layer(slab, 1, nx - 1),
            layer(flow, 2, nx - 1),
            layer(slab, 1, 0),
            layer(flow, 2, 0),
        ],
        out_specs=(whole((nx, cy, cz)), whole((2, nx, cz))),
    )(pulse, field, velocity, source, *prev, *nxt)


def on_device(adjoint, base_flow, source, pulse, actuator):
    count = lax.axis_size("tm")
    nt_loc, nx, cy, cz = adjoint.shape
    total = count * nt_loc
    chunk = nx * cy // count
    share = NACT // count
    pad = 8
    dmat = spectral_matrix(total)

    incoming = lax.all_to_all(adjoint.reshape(count, chunk, cz), "tm", 0, 0, tiled=True)

    field = adjoint[0]
    velocity = base_flow[:, 0]
    prev, nxt = neighbours((adjoint, base_flow), "space")
    kept, walls = stencil(pulse, field, velocity, source[0], prev, nxt)

    onehot = (actuator[:, :, None] == jnp.arange(NACT, dtype=jnp.int32)[None, None, :]).astype(
        jnp.float32
    )
    terms = jnp.dot(
        walls.reshape(2, -1),
        onehot.reshape(-1, NACT),
        precision=lax.Precision.HIGHEST,
        preferred_element_type=jnp.float32,
    )
    terms = butterfly_sum(terms, "space")
    scales = jnp.array([1.0, -pseudo_step * omega_rate], jnp.float32)[:, None] / total
    slices = jnp.transpose((terms * scales).reshape(2, count, share), (1, 0, 2))
    slices = jnp.pad(slices, ((0, 0), (0, 0), (0, cz - share)))
    pulse_row = jnp.broadcast_to(pulse.reshape(1, 1, 1), (count, 1, cz))
    grad_rows = jnp.concatenate([slices, pulse_row, jnp.zeros((count, pad - 3, cz), jnp.float32)], axis=1)
    kept, grad_rows, incoming = lax.optimization_barrier((kept, grad_rows, incoming))
    weighted = (-pseudo_step * omega_rate) * dmat
    derived = jnp.sum(weighted[:, :, None, None] * incoming[:, None], axis=0)

    outgoing = jnp.concatenate([derived, grad_rows], axis=1)
    incoming = lax.all_to_all(outgoing, "tm", 0, 0, tiled=True)
    scaled_term = incoming[:, :chunk].reshape(nx, cy, cz)
    cross = dmat[:, :, None] * incoming[None, :, chunk + 2, :] * incoming[:, None, chunk + 1, :]
    gradient = (jnp.sum(incoming[:, chunk, :], axis=0) + jnp.sum(cross, axis=(0, 1)))[:share]
    updated = kept + scaled_term
    return (updated[None], gradient)


def solution(mesh):
    in_specs = (
        P("tm", "space", None, None),
        P(None, "tm", "space", None, None),
        P("tm", "space", None, None),
        P("tm"),
        P("space", None),
    )
    out_specs = (P("tm", "space", None, None), P("tm"))
    return jax.shard_map(
        on_device, mesh=mesh, in_specs=in_specs, out_specs=out_specs, check_vma=False
    )
```
